512 devices in a mesh: req: 64 (over z, x, core), voc: 8 (over y).
Axes of the slice: x: 4, y: 8, z: 8, core: 2. Of those that a mesh axis runs over, the one named last changes fastest.
Arguments:
- hidden: bfloat16 [65536, 1600], P(('req', 'voc')), may hold values from -60 to 60
- norm_gain: float32 [1600], replicated, may hold values from 0.25 to 1.75
- unembed: bfloat16 [16384, 1600], P(('req', 'voc')), may hold values from -2 to 2
- targets: int32 [65536], P(('req', 'voc')), may hold values from 0 to 16383
- live: int32 [65536], P(('req', 'voc')), may hold values from 0 to 1, as said below
Outputs:
- logprob: float32 [65536], P(('req', 'voc'))
- entropy: float32 [65536], P(('req', 'voc'))
The draws below stay inside these ranges and needn't reach their ends.
Inputs may be any that keep to these rules, and one draw needn't show every extreme that they name: Within each aligned block of 1024 slots (one owner's) the live slots form a prefix of 128 to 1024 slots, and in every draw at least one block is wholly live.
All inputs are finite; a program needn't handle non-finite values.
Results may differ from the reference program's by a relative error of at most 0.0067.
Values may be sent and summed in bfloat16 or wider, within the bound.
No kernel may reach another device: no remote copies, remote signals or barrier semaphores. Data moves between devices by JAX's collectives and lax.ppermute only.
A program may use at most 64 MiB of HBM per device.

```python
import math
import jax
import jax.numpy as jnp
import numpy as np
from jax import lax

D = 1600
VOCAB = 16384
ROWS = 1024
TOKENS = 65536


def norm_level():
    return max(7.0, 240.0 / math.sqrt(D))


def entry_scale():
    return norm_level() / math.sqrt(D)


def drawn_places(key):
    offsets = jax.random.randint(jax.random.fold_in(key, 31), (8,), 0, VOCAB // 16)
    return jnp.arange(8, dtype=jnp.int32) * (VOCAB // 8) + 2 * offsets


def drawn_rows(key):
    base = jnp.clip(jax.random.normal(jax.random.fold_in(key, 33), (8, D), jnp.float32), -5.0, 5.0)
    return jnp.clip(base * entry_scale(), -2.0, 2.0)


def unembed_full(key):
    scale = entry_scale()
    base = jnp.clip(jax.random.normal(jax.random.fold_in(key, 7), (VOCAB, D), jnp.float32), -5.0, 5.0)
    table = jnp.clip(base * scale, -2.0, 2.0)
    places = drawn_places(key)
    leads = drawn_rows(key)
    noise = jnp.clip(jax.random.normal(jax.random.fold_in(key, 9), (8, D), jnp.float32), -3.0, 3.0) * (0.01 * scale)
    shrink = 1.0 - 2.5 / (norm_level() * math.sqrt(D))
    for pair in range(8):
        table = table.at[places[pair]].set(leads[pair])
        table = table.at[places[pair] + 1].set(jnp.clip(leads[pair] * shrink + noise[pair], -2.0, 2.0))
    return table


def draw_unembed(key, part):
    return unembed_full(key).astype(jnp.bfloat16)


def draw_hidden(key, part):
    base = jnp.clip(jax.random.normal(jax.random.fold_in(key, 11), (TOKENS, D), jnp.float32), -5.0, 5.0)
    leads = drawn_rows(key) / entry_scale()
    extra = jnp.clip(jax.random.normal(jax.random.fold_in(key, 14), (8, D), jnp.float32), -3.0, 3.0)
    for pair in range(8):
        mix = 0.86 + 0.02 * pair
        rest = math.sqrt(max(0.0, 1.0 - mix * mix))
        place = pair * (TOKENS // 8)
        base = base.at[place].set(6.0 * (mix * leads[pair] + rest * extra[pair]))
    return base.astype(jnp.bfloat16)


def draw_live(key, part):
    owners = TOKENS // ROWS
    spans = jax.random.randint(jax.random.fold_in(key, 3), (owners,), ROWS // 8, ROWS + 1)
    filled = jax.random.randint(jax.random.fold_in(key, 4), (), 0, owners)
    spans = jnp.where(jnp.arange(owners) == filled, ROWS, spans)
    slots = jnp.arange(TOKENS, dtype=jnp.int32)
    owner_of = slots // ROWS
    return (slots % ROWS < jnp.take(spans, owner_of)).astype(jnp.int32)


def plant(entries, key, low, top_value):
    shape = entries.shape
    index_at = [jax.random.randint(jax.random.fold_in(key, axis), (), 0, shape[axis]) for axis in range(len(shape))]
    entries = entries.at[tuple(index_at)].set(low)
    longest = shape.index(max(shape))
    index_at[longest] = (index_at[longest] + 1) % shape[longest]
    return entries.at[tuple(index_at)].set(top_value)


def rank_bounds(count, skew):
    weights = [(1 << 20) // math.isqrt(grade ** skew) + 1 for grade in range(1, count + 1)]
    scale = 1 + sum(weights) // (1 << 30)
    return np.cumsum(np.array([max(1, weight // scale) for weight in weights]))


def ranked(rng, shape, count, slope):
    listing = rank_bounds(count, slope)
    pick = jax.random.randint(jax.random.fold_in(rng, 1), shape, 0, int(listing[count - 1]))
    grade = jnp.searchsorted(jnp.asarray(listing, jnp.int32), pick, side="right")
    return jax.random.permutation(jax.random.fold_in(rng, 2), count)[grade].astype(jnp.int32)


def setup_inputs(seed: int = 0) -> dict:
    key_list = jax.random.split(jax.random.key(seed), 6)
    hidden = draw_hidden(jax.random.fold_in(key_list[5], 71), 0)
    norm_gain = jnp.clip(1.0 + 0.15 * jax.random.normal(key_list[1], (D,), jnp.float32), 0.25, 1.75)
    unembed = draw_unembed(jax.random.fold_in(key_list[5], 71), 0)
    targets = plant(ranked(key_list[3], (TOKENS,), VOCAB, 2), jax.random.fold_in(key_list[3], 3), 0, VOCAB - 1).astype(jnp.int32)
    live = draw_live(jax.random.fold_in(key_list[5], 71), 0)
    return dict(hidden=hidden, norm_gain=norm_gain, unembed=unembed, targets=targets, live=live)


def score_block(args, unembed):
    normed, wanted, alive = args
    logits = jnp.dot(normed, unembed.T, preferred_element_type=jnp.float32)
    top = lax.optimization_barrier(jnp.max(logits, axis=1))
    shifted = logits - top[:, None]
    weights = jnp.exp(shifted)
    total = lax.optimization_barrier(jnp.sum(weights, axis=1))
    spread = lax.optimization_barrier(jnp.sum(weights * shifted, axis=1))
    chosen = jnp.take_along_axis(logits, wanted[:, None].astype(jnp.int32), axis=1)[:, 0]
    mask = alive.astype(jnp.float32)
    logprob = (chosen - top - jnp.log(total)) * mask
    entropy = (jnp.log(total) - spread / total) * mask
    return (logprob, entropy)

def reference(hidden, norm_gain, unembed, targets, live):
    wide = hidden.astype(jnp.float32)
    normed = (wide * lax.rsqrt(lax.optimization_barrier(jnp.mean(wide * wide, axis=1, keepdims=True)) + 1e-06) * norm_gain).astype(jnp.bfloat16)
    blocks = TOKENS // ROWS
    logprob, entropy = lax.map(lambda args: score_block(args, unembed), (normed.reshape(blocks, ROWS, D), targets.reshape(blocks, ROWS), live.reshape(blocks, ROWS)))
    return (logprob.reshape(TOKENS), entropy.reshape(TOKENS))
```

```python
import jax
import jax.numpy as jnp
from jax import lax
from jax.sharding import Mesh, PartitionSpec as P

FLAT = ("z", "x", "c", "y")


def combine_stats(first, second):
    top = jnp.maximum(first[0], second[0])
    scale_one = jnp.exp(first[0] - top)
    scale_two = jnp.exp(second[0] - top)
    total = first[1] * scale_one + second[1] * scale_two
    spread = scale_one * (first[2] + (first[0] - top) * first[1]) + scale_two * (
        second[2] + (second[0] - top) * second[1]
    )
    return (top, total, spread, first[3] + second[3])


def shift(value, axis, size, step):
    return lax.ppermute(value, axis, [(i, (i + step) % size) for i in range(size)])


def chunk_stats(normed, piece, ids, wanted):
    logits = lax.dot_general(
        normed, piece, (((1,), (1,)), ((), ())), preferred_element_type=jnp.float32
    )
    chosen = jnp.sum(jnp.where(ids[None, :] == wanted[:, None], logits, 0.0), axis=1)
    fold_top = jnp.max(logits, axis=1)
    shifted = logits - fold_top[:, None]
    weights = jnp.exp(shifted)
    return (fold_top, jnp.sum(weights, axis=1), jnp.sum(weights * shifted, axis=1), chosen)


def on_device(hidden, norm_gain, unembed, targets, live):
    ny = lax.axis_size("y")
    nc = lax.axis_size("c")
    y = lax.axis_index("y")
    c = lax.axis_index("c")
    mine = hidden.shape[0]
    width = unembed.shape[0]

    wide = hidden.astype(jnp.float32)
    normed = (
        wide * lax.rsqrt(jnp.mean(wide * wide, axis=1, keepdims=True) + 1e-06) * norm_gain
    ).astype(jnp.bfloat16)

    blocks = [None] * ny
    blocks[0] = (normed, targets)
    fwd = ny // 2
    cur = (normed, targets)
    for d in range(1, fwd + 1):
        cur = shift(cur, "y", ny, 1)
        blocks[ny - d] = cur
    cur = (normed, targets)
    for d in range(1, ny - fwd):
        cur = shift(cur, "y", ny, -1)
        blocks[d] = cur
    rows = jnp.concatenate([b[0] for b in blocks], axis=0)
    wanted = jnp.concatenate([b[1] for b in blocks], axis=0)

    half = lax.all_gather(unembed, ("z", "x"), axis=0, tiled=True)
    other = shift(half, "c", nc, 1)

    def ids_of(core):
        local = jnp.arange(half.shape[0], dtype=jnp.int32)
        return ((local // width) * (nc * ny) + core * ny + y) * width + local % width

    count = rows.shape[0]
    zeros = jnp.zeros((count,), jnp.float32)
    stats = (jnp.full((count,), -1e30, jnp.float32), zeros, zeros, zeros)
    step = min(512, half.shape[0])
    for table, core in ((half, c), (other, (c + 1) % nc)):
        ids = ids_of(core)
        for first in range(0, table.shape[0], step):
            stats = combine_stats(
                stats,
                chunk_stats(rows, table[first : first + step], ids[first : first + step], wanted),
            )

    packed = jnp.stack(stats).reshape(4, ny, mine)
    merged = tuple(packed[:, 0])
    for d in range(1, ny):
        got = shift(packed[:, d], "y", ny, d)
        merged = combine_stats(merged, tuple(got))
    top, total, spread, picked = merged
    mask = live.astype(jnp.float32)
    logprob = (picked - top - jnp.log(total)) * mask
    entropy = (jnp.log(total) - spread / total) * mask
    return (logprob, entropy)


def solution(mesh):
    nz, nx, nc = 8, 4, 2
    ny = mesh.devices.shape[1]
    req = mesh.devices.shape[0]
    nz = req // (nx * nc)
    flat = Mesh(mesh.devices.reshape(nz, nx, nc, ny), FLAT)
    return jax.shard_map(
        on_device,
        mesh=flat,
        in_specs=(P(FLAT, None), P(), P(FLAT, None), P(FLAT), P(FLAT)),
        out_specs=(P(FLAT), P(FLAT)),
        check_vma=False,
    )
```

```python
import jax
import jax.numpy as jnp
from jax import lax
from jax.sharding import Mesh, PartitionSpec as P

FLAT = ("z", "x", "c", "y")


def combine_stats(first, second):
    top = jnp.maximum(first[0], second[0])
    scale_one = jnp.exp(first[0] - top)
    scale_two = jnp.exp(second[0] - top)
    total = first[1] * scale_one + second[1] * scale_two
    spread = scale_one * (first[2] + (first[0] - top) * first[1]) + scale_two * (
        second[2] + (second[0] - top) * second[1]
    )
    return (top, total, spread, first[3] + second[3])


def shift(value, axis, size, step):
    return lax.ppermute(value, axis, [(i, (i + step) % size) for i in range(size)])


def chunk_stats(normed, piece, ids, wanted):
    logits = lax.dot_general(
        normed, piece, (((1,), (1,)), ((), ())), preferred_element_type=jnp.float32
    )
    chosen = jnp.sum(jnp.where(ids[None, :] == wanted[:, None], logits, 0.0), axis=1)
    fold_top = jnp.max(logits, axis=1)
    shifted = logits - fold_top[:, None]
    weights = jnp.exp(shifted)
    return (fold_top, jnp.sum(weights, axis=1), jnp.sum(weights * shifted, axis=1), chosen)


def on_device(hidden, norm_gain, unembed, targets, live):
    ny = lax.axis_size("y")
    nc = lax.axis_size("c")
    y = lax.axis_index("y")
    c = lax.axis_index("c")
    mine = hidden.shape[0]
    dim = hidden.shape[1]
    width = unembed.shape[0]

    wide = hidden.astype(jnp.float32)
    normed = (
        wide * lax.rsqrt(jnp.mean(wide * wide, axis=1, keepdims=True) + 1e-06) * norm_gain
    ).astype(jnp.bfloat16)

    code = jnp.zeros((mine, 16), jnp.bfloat16)
    code = code.at[:, 0].set((targets // 128).astype(jnp.bfloat16))
    code = code.at[:, 1].set((targets % 128).astype(jnp.bfloat16))
    block = jnp.concatenate([normed, code], axis=1)

    blocks = [None] * ny
    blocks[0] = block
    fwd = ny // 2
    cur = block
    for d in range(1, fwd + 1):
        cur = shift(cur, "y", ny, 1)
        blocks[ny - d] = cur
    cur = block
    for d in range(1, ny - fwd):
        cur = shift(cur, "y", ny, -1)
        blocks[d] = cur
    rows = jnp.concatenate([b[:, :dim] for b in blocks], axis=0)
    wanted = jnp.concatenate(
        [b[:, dim].astype(jnp.int32) * 128 + b[:, dim + 1].astype(jnp.int32) for b in blocks], axis=0
    )

    whole = lax.all_gather(unembed, ("z", "x", "c"), axis=0, tiled=True)
    local = jnp.arange(whole.shape[0], dtype=jnp.int32)
    ids = ((local // width) * ny + y) * width + local % width

    count = rows.shape[0]
    zeros = jnp.zeros((count,), jnp.float32)
    stats = (jnp.full((count,), -1e30, jnp.float32), zeros, zeros, zeros)
    step = min(512, whole.shape[0])
    for first in range(0, whole.shape[0], step):
        stats = combine_stats(
            stats,
            chunk_stats(rows, whole[first : first + step], ids[first : first + step], wanted),
        )

    packed = jnp.roll(jnp.stack(stats).reshape(4, ny, mine), y, axis=1).reshape(4, ny * mine)
    got = lax.all_to_all(packed, "y", 1, 1, tiled=True).reshape(4, ny, mine)
    tops, totals, spreads, chosen = got[0], got[1], got[2], got[3]
    top = jnp.max(tops, axis=0)
    scale = jnp.exp(tops - top[None])
    total = jnp.sum(totals * scale, axis=0)
    spread = jnp.sum(scale * (spreads + (tops - top[None]) * totals), axis=0)
    picked = jnp.sum(chosen, axis=0)
    mask = live.astype(jnp.float32)
    logprob = (picked - top - jnp.log(total)) * mask
    entropy = (jnp.log(total) - spread / total) * mask
    return (logprob, entropy)


def solution(mesh):
    nz, nx, nc = 8, 4, 2
    ny = mesh.devices.shape[1]
    req = mesh.devices.shape[0]
    nz = req // (nx * nc)
    flat = Mesh(mesh.devices.reshape(nz, nx, nc, ny), FLAT)
    return jax.shard_map(
        on_device,
        mesh=flat,
        in_specs=(P(FLAT, None), P(), P(FLAT, None), P(FLAT), P(FLAT)),
        out_specs=(P(FLAT), P(FLAT)),
        check_vma=False,
    )
```

```python
import jax
import jax.numpy as jnp
from jax import lax
from jax.sharding import Mesh, PartitionSpec as P

FLAT = ("z", "x", "c", "y")


def combine_stats(first, second):
    top = jnp.maximum(first[0], second[0])
    scale_one = jnp.exp(first[0] - top)
    scale_two = jnp.exp(second[0] - top)
    total = first[1] * scale_one + second[1] * scale_two
    spread = scale_one * (first[2] + (first[0] - top) * first[1]) + scale_two * (
        second[2] + (second[0] - top) * second[1]
    )
    return (top, total, spread, first[3] + second[3])


def shift(value, axis, size, step):
    return lax.ppermute(value, axis, [(i, (i + step) % size) for i in range(size)])


def chunk_stats(normed, piece, ids, wanted):
    logits = lax.dot_general(
        normed, piece, (((1,), (1,)), ((), ())), preferred_element_type=jnp.float32
    )
    chosen = jnp.sum(jnp.where(ids[None, :] == wanted[:, None], logits, 0.0), axis=1)
    fold_top = jnp.max(logits, axis=1)
    shifted = logits - fold_top[:, None]
    weights = jnp.exp(shifted)
    return (fold_top, jnp.sum(weights, axis=1), jnp.sum(weights * shifted, axis=1), chosen)


def on_device(hidden, norm_gain, unembed, targets, live):
    ny = lax.axis_size("y")
    nc = lax.axis_size("c")
    y = lax.axis_index("y")
    c = lax.axis_index("c")
    mine = hidden.shape[0]
    dim = hidden.shape[1]
    width = unembed.shape[0]

    wide = hidden.astype(jnp.float32)
    normed = (
        wide * lax.rsqrt(jnp.mean(wide * wide, axis=1, keepdims=True) + 1e-06) * norm_gain
    ).astype(jnp.bfloat16)

    code = jnp.zeros((mine, 16), jnp.bfloat16)
    code = code.at[:, 0].set((targets // 128).astype(jnp.bfloat16))
    code = code.at[:, 1].set((targets % 128).astype(jnp.bfloat16))
    block = jnp.concatenate([normed, code], axis=1)

    blocks = [None] * ny
    blocks[0] = block
    fwd = ny // 2
    cur = block
    for d in range(1, fwd + 1):
        cur = shift(cur, "y", ny, 1)
        blocks[ny - d] = cur
    cur = block
    for d in range(1, ny - fwd):
        cur = shift(cur, "y", ny, -1)
        blocks[d] = cur
    rows = jnp.concatenate([b[:, :dim] for b in blocks], axis=0)
    wanted = jnp.concatenate(
        [b[:, dim].astype(jnp.int32) * 128 + b[:, dim + 1].astype(jnp.int32) for b in blocks], axis=0
    )

    whole = lax.all_gather(unembed, ("z", "x", "c"), axis=0, tiled=True)
    local = jnp.arange(whole.shape[0], dtype=jnp.int32)
    ids = ((local // width) * ny + y) * width + local % width

    parts = 2
    part = mine // parts
    step = min(512, whole.shape[0])
    rows3 = rows.reshape(ny, mine, dim)
    wanted3 = wanted.reshape(ny, mine)
    results = []
    for h in range(parts):
        sub = rows3[:, h * part : (h + 1) * part].reshape(ny * part, dim)
        if results:
            results[-1], sub = lax.optimization_barrier((results[-1], sub))
        sub_wanted = wanted3[:, h * part : (h + 1) * part].reshape(ny * part)
        count = sub.shape[0]
        zeros = jnp.zeros((count,), jnp.float32)
        stats = (jnp.full((count,), -1e30, jnp.float32), zeros, zeros, zeros)
        for first in range(0, whole.shape[0], step):
            stats = combine_stats(
                stats,
                chunk_stats(sub, whole[first : first + step], ids[first : first + step], sub_wanted),
            )
        packed = jnp.roll(jnp.stack(stats).reshape(4, ny, part), y, axis=1).reshape(4, ny * part)
        results.append(packed)
    results = [lax.all_to_all(p, "y", 1, 1, tiled=True).reshape(4, ny, part) for p in results]
    got = jnp.concatenate(results, axis=2)
    tops, totals, spreads, chosen = got[0], got[1], got[2], got[3]
    top = jnp.max(tops, axis=0)
    scale = jnp.exp(tops - top[None])
    total = jnp.sum(totals * scale, axis=0)
    spread = jnp.sum(scale * (spreads + (tops - top[None]) * totals), axis=0)
    picked = jnp.sum(chosen, axis=0)
    mask = live.astype(jnp.float32)
    logprob = (picked - top - jnp.log(total)) * mask
    entropy = (jnp.log(total) - spread / total) * mask
    return (logprob, entropy)


def solution(mesh):
    nz, nx, nc = 8, 4, 2
    ny = mesh.devices.shape[1]
    req = mesh.devices.shape[0]
    nz = req // (nx * nc)
    flat = Mesh(mesh.devices.reshape(nz, nx, nc, ny), FLAT)
    return jax.shard_map(
        on_device,
        mesh=flat,
        in_specs=(P(FLAT, None), P(), P(FLAT, None), P(FLAT), P(FLAT)),
        out_specs=(P(FLAT), P(FLAT)),
        check_vma=False,
    )
```

```python
import jax
import jax.numpy as jnp
from jax import lax
from jax.experimental import pallas as pl
from jax.sharding import Mesh, PartitionSpec as P

FLAT = ("z", "x", "c", "y")


def combine_stats(first, second):
    top = jnp.maximum(first[0], second[0])
    scale_one = jnp.exp(first[0] - top)
    scale_two = jnp.exp(second[0] - top)
    total = first[1] * scale_one + second[1] * scale_two
    spread = scale_one * (first[2] + (first[0] - top) * first[1]) + scale_two * (
        second[2] + (second[0] - top) * second[1]
    )
    return (top, total, spread, first[3] + second[3])


def shift(value, axis, size, step):
    return lax.ppermute(value, axis, [(i, (i + step) % size) for i in range(size)])


def chunk_stats(normed, piece, ids, wanted):
    logits = lax.dot_general(
        normed, piece, (((1,), (1,)), ((), ())), preferred_element_type=jnp.float32
    )
    chosen = jnp.sum(jnp.where(ids[None, :] == wanted[:, None], logits, 0.0), axis=1)
    fold_top = jnp.max(logits, axis=1)
    shifted = logits - fold_top[:, None]
    weights = jnp.exp(shifted)
    return (fold_top, jnp.sum(weights, axis=1), jnp.sum(weights * shifted, axis=1), chosen)


def stats_kernel(rows_ref, vocab_ref, wanted_ref, ids_ref, top_ref, total_ref, spread_ref, chosen_ref):
    j = pl.program_id(0)

    @pl.when(j == 0)
    def _():
        top_ref[...] = jnp.full(top_ref.shape, -1e30, jnp.float32)
        total_ref[...] = jnp.zeros(total_ref.shape, jnp.float32)
        spread_ref[...] = jnp.zeros(spread_ref.shape, jnp.float32)
        chosen_ref[...] = jnp.zeros(chosen_ref.shape, jnp.float32)

    logits = lax.dot_general(
        rows_ref[...], vocab_ref[...], (((1,), (1,)), ((), ())), preferred_element_type=jnp.float32
    )
    hit = ids_ref[...] == wanted_ref[...]
    chosen_ref[...] += jnp.sum(jnp.where(hit, logits, 0.0), axis=1, keepdims=True)
    fold = jnp.max(logits, axis=1, keepdims=True)
    shifted = logits - fold
    weights = jnp.exp(shifted)
    new_total = jnp.sum(weights, axis=1, keepdims=True)
    new_spread = jnp.sum(weights * shifted, axis=1, keepdims=True)
    old_top = top_ref[...]
    top = jnp.maximum(old_top, fold)
    scale_one = jnp.exp(old_top - top)
    scale_two = jnp.exp(fold - top)
    old_total = total_ref[...]
    total_ref[...] = old_total * scale_one + new_total * scale_two
    spread_ref[...] = scale_one * (spread_ref[...] + (old_top - top) * old_total) + scale_two * (
        new_spread + (fold - top) * new_total
    )
    top_ref[...] = top


def row_stats(rows, vocab, wanted, ids, tile=256):
    count, dim = rows.shape
    width = vocab.shape[0]
    col = pl.BlockSpec((count, 1), lambda j: (0, 0))
    outs = pl.pallas_call(
        stats_kernel,
        grid=(width // tile,),
        in_specs=[
            pl.BlockSpec((count, dim), lambda j: (0, 0)),
            pl.BlockSpec((tile, dim), lambda j: (j, 0)),
            col,
            pl.BlockSpec((1, tile), lambda j: (0, j)),
        ],
        out_specs=[col, col, col, col],
        out_shape=[jax.ShapeDtypeStruct((count, 1), jnp.float32)] * 4,
        cost_estimate=pl.CostEstimate(
            flops=2 * count * width * dim,
            transcendentals=count * width,
            bytes_accessed=2 * (count + width) * dim,
        ),
    )(rows, vocab, wanted.reshape(count, 1), ids.reshape(1, width))
    return tuple(o[:, 0] for o in outs)


def on_device(hidden, norm_gain, unembed, targets, live):
    ny = lax.axis_size("y")
    nc = lax.axis_size("c")
    y = lax.axis_index("y")
    c = lax.axis_index("c")
    mine = hidden.shape[0]
    dim = hidden.shape[1]
    width = unembed.shape[0]

    wide = hidden.astype(jnp.float32)
    normed = (
        wide * lax.rsqrt(jnp.mean(wide * wide, axis=1, keepdims=True) + 1e-06) * norm_gain
    ).astype(jnp.bfloat16)

    code = jnp.zeros((mine, 16), jnp.bfloat16)
    code = code.at[:, 0].set((targets // 128).astype(jnp.bfloat16))
    code = code.at[:, 1].set((targets % 128).astype(jnp.bfloat16))
    block = jnp.concatenate([normed, code], axis=1)

    blocks = [None] * ny
    blocks[0] = block
    fwd = ny // 2
    cur = block
    for d in range(1, fwd + 1):
        cur = shift(cur, "y", ny, 1)
        blocks[ny - d] = cur
    cur = block
    for d in range(1, ny - fwd):
        cur = shift(cur, "y", ny, -1)
        blocks[d] = cur
    rows = jnp.concatenate([b[:, :dim] for b in blocks], axis=0)
    wanted = jnp.concatenate(
        [b[:, dim].astype(jnp.int32) * 128 + b[:, dim + 1].astype(jnp.int32) for b in blocks], axis=0
    )

    whole = lax.all_gather(unembed, ("z", "x", "c"), axis=0, tiled=True)
    local = jnp.arange(whole.shape[0], dtype=jnp.int32)
    ids = ((local // width) * ny + y) * width + local % width

    stats = row_stats(rows, whole, wanted, ids)

    packed = jnp.roll(jnp.stack(stats).reshape(4, ny, mine), y, axis=1).reshape(4, ny * mine)
    got = lax.all_to_all(packed, "y", 1, 1, tiled=True).reshape(4, ny, mine)
    tops, totals, spreads, chosen = got[0], got[1], got[2], got[3]
    top = jnp.max(tops, axis=0)
    scale = jnp.exp(tops - top[None])
    total = jnp.sum(totals * scale, axis=0)
    spread = jnp.sum(scale * (spreads + (tops - top[None]) * totals), axis=0)
    picked = jnp.sum(chosen, axis=0)
    mask = live.astype(jnp.float32)
    logprob = (picked - top - jnp.log(total)) * mask
    entropy = (jnp.log(total) - spread / total) * mask
    return (logprob, entropy)


def solution(mesh):
    nz, nx, nc = 8, 4, 2
    ny = mesh.devices.shape[1]
    req = mesh.devices.shape[0]
    nz = req // (nx * nc)
    flat = Mesh(mesh.devices.reshape(nz, nx, nc, ny), FLAT)
    return jax.shard_map(
        on_device,
        mesh=flat,
        in_specs=(P(FLAT, None), P(), P(FLAT, None), P(FLAT), P(FLAT)),
        out_specs=(P(FLAT), P(FLAT)),
        check_vma=False,
    )
```

```python
import jax
import jax.numpy as jnp
from jax import lax
from jax.experimental import pallas as pl
from jax.sharding import Mesh, PartitionSpec as P

FLAT = ("z", "x", "c", "y")


def combine_stats(first, second):
    top = jnp.maximum(first[0], second[0])
    scale_one = jnp.exp(first[0] - top)
    scale_two = jnp.exp(second[0] - top)
    total = first[1] * scale_one + second[1] * scale_two
    spread = scale_one * (first[2] + (first[0] - top) * first[1]) + scale_two * (
        second[2] + (second[0] - top) * second[1]
    )
    return (top, total, spread, first[3] + second[3])


def shift(value, axis, size, step):
    return lax.ppermute(value, axis, [(i, (i + step) % size) for i in range(size)])


def chunk_stats(normed, piece, ids, wanted):
    logits = lax.dot_general(
        normed, piece, (((1,), (1,)), ((), ())), preferred_element_type=jnp.float32
    )
    chosen = jnp.sum(jnp.where(ids[None, :] == wanted[:, None], logits, 0.0), axis=1)
    fold_top = jnp.max(logits, axis=1)
    shifted = logits - fold_top[:, None]
    weights = jnp.exp(shifted)
    return (fold_top, jnp.sum(weights, axis=1), jnp.sum(weights * shifted, axis=1), chosen)


def stats_kernel(rows_ref, vocab_ref, wanted_ref, ids_ref, top_ref, total_ref, spread_ref, chosen_ref):
    j = pl.program_id(0)

    @pl.when(j == 0)
    def _():
        top_ref[...] = jnp.full(top_ref.shape, -1e30, jnp.float32)
        total_ref[...] = jnp.zeros(total_ref.shape, jnp.float32)
        spread_ref[...] = jnp.zeros(spread_ref.shape, jnp.float32)
        chosen_ref[...] = jnp.zeros(chosen_ref.shape, jnp.float32)

    logits = lax.dot_general(
        vocab_ref[...], rows_ref[...], (((1,), (1,)), ((), ())), preferred_element_type=jnp.float32
    )
    hit = ids_ref[...] == wanted_ref[...]
    chosen_ref[...] += jnp.sum(jnp.where(hit, logits, 0.0), axis=0, keepdims=True)
    fold = jnp.max(logits, axis=0, keepdims=True)
    shifted = logits - fold
    weights = jnp.exp(shifted)
    new_total = jnp.sum(weights, axis=0, keepdims=True)
    new_spread = jnp.sum(weights * shifted, axis=0, keepdims=True)
    old_top = top_ref[...]
    top = jnp.maximum(old_top, fold)
    scale_one = jnp.exp(old_top - top)
    scale_two = jnp.exp(fold - top)
    old_total = total_ref[...]
    total_ref[...] = old_total * scale_one + new_total * scale_two
    spread_ref[...] = scale_one * (spread_ref[...] + (old_top - top) * old_total) + scale_two * (
        new_spread + (fold - top) * new_total
    )
    top_ref[...] = top


def row_stats(rows, vocab, wanted, ids, tile=256):
    count, dim = rows.shape
    width = vocab.shape[0]
    line = pl.BlockSpec((1, count), lambda j: (0, 0))
    outs = pl.pallas_call(
        stats_kernel,
        grid=(width // tile,),
        in_specs=[
            pl.BlockSpec((count, dim), lambda j: (0, 0)),
            pl.BlockSpec((tile, dim), lambda j: (j, 0)),
            line,
            pl.BlockSpec((tile, 1), lambda j: (j, 0)),
        ],
        out_specs=[line, line, line, line],
        out_shape=[jax.ShapeDtypeStruct((1, count), jnp.float32)] * 4,
        cost_estimate=pl.CostEstimate(
            flops=2 * count * width * dim,
            transcendentals=count * width,
            bytes_accessed=2 * (count + width) * dim,
        ),
    )(rows, vocab, wanted.reshape(1, count), ids.reshape(width, 1))
    return tuple(o.reshape(count) for o in outs)


def on_device(hidden, norm_gain, unembed, targets, live):
    ny = lax.axis_size("y")
    nc = lax.axis_size("c")
    y = lax.axis_index("y")
    c = lax.axis_index("c")
    mine = hidden.shape[0]
    dim = hidden.shape[1]
    width = unembed.shape[0]

    wide = hidden.astype(jnp.float32)
    normed = (
        wide * lax.rsqrt(jnp.mean(wide * wide, axis=1, keepdims=True) + 1e-06) * norm_gain
    ).astype(jnp.bfloat16)

    code = jnp.zeros((mine, 16), jnp.bfloat16)
    code = code.at[:, 0].set((targets // 128).astype(jnp.bfloat16))
    code = code.at[:, 1].set((targets % 128).astype(jnp.bfloat16))
    block = jnp.concatenate([normed, code], axis=1)

    blocks = [None] * ny
    blocks[0] = block
    fwd = ny // 2
    cur = block
    for d in range(1, fwd + 1):
        cur = shift(cur, "y", ny, 1)
        blocks[ny - d] = cur
    cur = block
    for d in range(1, ny - fwd):
        cur = shift(cur, "y", ny, -1)
        blocks[d] = cur
    rows = jnp.concatenate([b[:, :dim] for b in blocks], axis=0)
    wanted = jnp.concatenate(
        [b[:, dim].astype(jnp.int32) * 128 + b[:, dim + 1].astype(jnp.int32) for b in blocks], axis=0
    )

    whole = lax.all_gather(unembed, ("z", "x", "c"), axis=0, tiled=True)
    local = jnp.arange(whole.shape[0], dtype=jnp.int32)
    ids = ((local // width) * ny + y) * width + local % width

    stats = row_stats(rows, whole, wanted, ids)

    packed = jnp.roll(jnp.stack(stats).reshape(4, ny, mine), y, axis=1).reshape(4, ny * mine)
    got = lax.all_to_all(packed, "y", 1, 1, tiled=True).reshape(4, ny, mine)
    tops, totals, spreads, chosen = got[0], got[1], got[2], got[3]
    top = jnp.max(tops, axis=0)
    scale = jnp.exp(tops - top[None])
    total = jnp.sum(totals * scale, axis=0)
    spread = jnp.sum(scale * (spreads + (tops - top[None]) * totals), axis=0)
    picked = jnp.sum(chosen, axis=0)
    mask = live.astype(jnp.float32)
    logprob = (picked - top - jnp.log(total)) * mask
    entropy = (jnp.log(total) - spread / total) * mask
    return (logprob, entropy)


def solution(mesh):
    nz, nx, nc = 8, 4, 2
    ny = mesh.devices.shape[1]
    req = mesh.devices.shape[0]
    nz = req // (nx * nc)
    flat = Mesh(mesh.devices.reshape(nz, nx, nc, ny), FLAT)
    return jax.shard_map(
        on_device,
        mesh=flat,
        in_specs=(P(FLAT, None), P(), P(FLAT, None), P(FLAT), P(FLAT)),
        out_specs=(P(FLAT), P(FLAT)),
        check_vma=False,
    )
```

```python
import jax
import jax.numpy as jnp
from jax import lax
from jax.experimental import pallas as pl
from jax.sharding import Mesh, PartitionSpec as P

FLAT = ("z", "x", "c", "y")


def combine_stats(first, second):
    top = jnp.maximum(first[0], second[0])
    scale_one = jnp.exp(first[0] - top)
    scale_two = jnp.exp(second[0] - top)
    total = first[1] * scale_one + second[1] * scale_two
    spread = scale_one * (first[2] + (first[0] - top) * first[1]) + scale_two * (
        second[2] + (second[0] - top) * second[1]
    )
    return (top, total, spread, first[3] + second[3])


def shift(value, axis, size, step):
    return lax.ppermute(value, axis, [(i, (i + step) % size) for i in range(size)])


def chunk_stats(normed, piece, ids, wanted):
    logits = lax.dot_general(
        normed, piece, (((1,), (1,)), ((), ())), preferred_element_type=jnp.float32
    )
    chosen = jnp.sum(jnp.where(ids[None, :] == wanted[:, None], logits, 0.0), axis=1)
    fold_top = jnp.max(logits, axis=1)
    shifted = logits - fold_top[:, None]
    weights = jnp.exp(shifted)
    return (fold_top, jnp.sum(weights, axis=1), jnp.sum(weights * shifted, axis=1), chosen)


def stats_kernel(rows_ref, vocab_ref, wanted_ref, ids_ref, top_ref, total_ref, spread_ref, chosen_ref):
    j = pl.program_id(0)

    @pl.when(j == 0)
    def _():
        top_ref[...] = jnp.full(top_ref.shape, -1e30, jnp.float32)
        total_ref[...] = jnp.zeros(total_ref.shape, jnp.float32)
        spread_ref[...] = jnp.zeros(spread_ref.shape, jnp.float32)
        chosen_ref[...] = jnp.zeros(chosen_ref.shape, jnp.float32)

    logits = lax.dot_general(
        vocab_ref[...], rows_ref[...], (((1,), (1,)), ((), ())), preferred_element_type=jnp.float32
    )
    hit = ids_ref[...] == wanted_ref[...]
    chosen_ref[...] += jnp.sum(jnp.where(hit, logits, 0.0), axis=0, keepdims=True)
    fold = jnp.max(logits, axis=0, keepdims=True)
    shifted = logits - fold
    weights = jnp.exp(shifted)
    new_total = jnp.sum(weights, axis=0, keepdims=True)
    new_spread = jnp.sum(weights * shifted, axis=0, keepdims=True)
    old_top = top_ref[...]
    top = jnp.maximum(old_top, fold)
    scale_one = jnp.exp(old_top - top)
    scale_two = jnp.exp(fold - top)
    old_total = total_ref[...]
    total_ref[...] = old_total * scale_one + new_total * scale_two
    spread_ref[...] = scale_one * (spread_ref[...] + (old_top - top) * old_total) + scale_two * (
        new_spread + (fold - top) * new_total
    )
    top_ref[...] = top


def row_stats(rows, vocab, wanted, ids, tile=256):
    count, dim = rows.shape
    width = vocab.shape[0]
    line = pl.BlockSpec((1, count), lambda j: (0, 0))
    outs = pl.pallas_call(
        stats_kernel,
        grid=(width // tile,),
        in_specs=[
            pl.BlockSpec((count, dim), lambda j: (0, 0)),
            pl.BlockSpec((tile, dim), lambda j: (j, 0)),
            line,
            pl.BlockSpec((tile, 1), lambda j: (j, 0)),
        ],
        out_specs=[line, line, line, line],
        out_shape=[jax.ShapeDtypeStruct((1, count), jnp.float32)] * 4,
        cost_estimate=pl.CostEstimate(
            flops=2 * count * width * dim,
            transcendentals=count * width,
            bytes_accessed=2 * (count + width) * dim,
        ),
    )(rows, vocab, wanted.reshape(1, count), ids.reshape(width, 1))
    return tuple(o.reshape(count) for o in outs)


def on_device(hidden, norm_gain, unembed, targets, live):
    ny = lax.axis_size("y")
    nc = lax.axis_size("c")
    y = lax.axis_index("y")
    c = lax.axis_index("c")
    mine = hidden.shape[0]
    dim = hidden.shape[1]
    width = unembed.shape[0]

    wide = hidden.astype(jnp.float32)
    normed = (
        wide * lax.rsqrt(jnp.mean(wide * wide, axis=1, keepdims=True) + 1e-06) * norm_gain
    ).astype(jnp.bfloat16)

    code = jnp.zeros((mine, 16), jnp.bfloat16)
    code = code.at[:, 0].set((targets // 128).astype(jnp.bfloat16))
    code = code.at[:, 1].set((targets % 128).astype(jnp.bfloat16))
    block = jnp.concatenate([normed, code], axis=1)

    blocks = [None] * ny
    blocks[0] = block
    fwd = ny // 2
    cur = block
    for d in range(1, fwd + 1):
        cur = shift(cur, "y", ny, 1)
        blocks[ny - d] = cur
    cur = block
    for d in range(1, ny - fwd):
        cur = shift(cur, "y", ny, -1)
        blocks[d] = cur
    rows = jnp.concatenate([b[:, :dim] for b in blocks], axis=0)
    wanted = jnp.concatenate(
        [b[:, dim].astype(jnp.int32) * 128 + b[:, dim + 1].astype(jnp.int32) for b in blocks], axis=0
    )

    nx = lax.axis_size("x")
    x = lax.axis_index("x")
    near = [None] * nx
    near[0] = unembed
    cur = unembed
    for d in range(1, nx // 2 + 1):
        cur = shift(cur, "x", nx, 1)
        near[nx - d] = cur
    cur = unembed
    for d in range(1, nx - nx // 2):
        cur = shift(cur, "x", nx, -1)
        near[d] = cur
    whole = lax.all_gather(jnp.concatenate(near, axis=0), ("z", "c"), axis=0, tiled=True)
    local = jnp.arange(whole.shape[0], dtype=jnp.int32)
    group, place = local // (nx * width), local % (nx * width)
    far_z, far_c = group // nc, group % nc
    far_x = (x + place // width) % nx
    ids = (((far_z * nx + far_x) * nc + far_c) * ny + y) * width + place % width

    stats = row_stats(rows, whole, wanted, ids)

    packed = jnp.roll(jnp.stack(stats).reshape(4, ny, mine), y, axis=1).reshape(4, ny * mine)
    got = lax.all_to_all(packed, "y", 1, 1, tiled=True).reshape(4, ny, mine)
    tops, totals, spreads, chosen = got[0], got[1], got[2], got[3]
    top = jnp.max(tops, axis=0)
    scale = jnp.exp(tops - top[None])
    total = jnp.sum(totals * scale, axis=0)
    spread = jnp.sum(scale * (spreads + (tops - top[None]) * totals), axis=0)
    picked = jnp.sum(chosen, axis=0)
    mask = live.astype(jnp.float32)
    logprob = (picked - top - jnp.log(total)) * mask
    entropy = (jnp.log(total) - spread / total) * mask
    return (logprob, entropy)


def solution(mesh):
    nz, nx, nc = 8, 4, 2
    ny = mesh.devices.shape[1]
    req = mesh.devices.shape[0]
    nz = req // (nx * nc)
    flat = Mesh(mesh.devices.reshape(nz, nx, nc, ny), FLAT)
    return jax.shard_map(
        on_device,
        mesh=flat,
        in_specs=(P(FLAT, None), P(), P(FLAT, None), P(FLAT), P(FLAT)),
        out_specs=(P(FLAT), P(FLAT)),
        check_vma=False,
    )
```

```python
import jax
import jax.numpy as jnp
from jax import lax
from jax.experimental import pallas as pl
from jax.sharding import Mesh, PartitionSpec as P

FLAT = ("z", "x", "c", "y")


def combine_stats(first, second):
    top = jnp.maximum(first[0], second[0])
    scale_one = jnp.exp(first[0] - top)
    scale_two = jnp.exp(second[0] - top)
    total = first[1] * scale_one + second[1] * scale_two
    spread = scale_one * (first[2] + (first[0] - top) * first[1]) + scale_two * (
        second[2] + (second[0] - top) * second[1]
    )
    return (top, total, spread, first[3] + second[3])


def shift(value, axis, size, step):
    return lax.ppermute(value, axis, [(i, (i + step) % size) for i in range(size)])


def chunk_stats(normed, piece, ids, wanted):
    logits = lax.dot_general(
        normed, piece, (((1,), (1,)), ((), ())), preferred_element_type=jnp.float32
    )
    chosen = jnp.sum(jnp.where(ids[None, :] == wanted[:, None], logits, 0.0), axis=1)
    fold_top = jnp.max(logits, axis=1)
    shifted = logits - fold_top[:, None]
    weights = jnp.exp(shifted)
    return (fold_top, jnp.sum(weights, axis=1), jnp.sum(weights * shifted, axis=1), chosen)


def stats_kernel(rows_ref, vocab_ref, wanted_ref, ids_ref, top_ref, total_ref, spread_ref, chosen_ref):
    j = pl.program_id(0)

    @pl.when(j == 0)
    def _():
        top_ref[...] = jnp.full(top_ref.shape, -1e30, jnp.float32)
        total_ref[...] = jnp.zeros(total_ref.shape, jnp.float32)
        spread_ref[...] = jnp.zeros(spread_ref.shape, jnp.float32)
        chosen_ref[...] = jnp.zeros(chosen_ref.shape, jnp.float32)

    logits = lax.dot_general(
        vocab_ref[...], rows_ref[...], (((1,), (1,)), ((), ())), preferred_element_type=jnp.float32
    )
    hit = ids_ref[...] == wanted_ref[...]
    chosen_ref[...] += jnp.sum(jnp.where(hit, logits, 0.0), axis=0, keepdims=True)
    fold = jnp.max(logits, axis=0, keepdims=True)
    shifted = logits - fold
    weights = jnp.exp(shifted)
    new_total = jnp.sum(weights, axis=0, keepdims=True)
    new_spread = jnp.sum(weights * shifted, axis=0, keepdims=True)
    old_top = top_ref[...]
    top = jnp.maximum(old_top, fold)
    scale_one = jnp.exp(old_top - top)
    scale_two = jnp.exp(fold - top)
    old_total = total_ref[...]
    total_ref[...] = old_total * scale_one + new_total * scale_two
    spread_ref[...] = scale_one * (spread_ref[...] + (old_top - top) * old_total) + scale_two * (
        new_spread + (fold - top) * new_total
    )
    top_ref[...] = top


def row_stats(rows, vocab, wanted, ids, tile=256):
    count, dim = rows.shape
    width = vocab.shape[0]
    line = pl.BlockSpec((1, count), lambda j: (0, 0))
    outs = pl.pallas_call(
        stats_kernel,
        grid=(width // tile,),
        in_specs=[
            pl.BlockSpec((count, dim), lambda j: (0, 0)),
            pl.BlockSpec((tile, dim), lambda j: (j, 0)),
            line,
            pl.BlockSpec((tile, 1), lambda j: (j, 0)),
        ],
        out_specs=[line, line, line, line],
        out_shape=[jax.ShapeDtypeStruct((1, count), jnp.float32)] * 4,
        cost_estimate=pl.CostEstimate(
            flops=2 * count * width * dim,
            transcendentals=count * width,
            bytes_accessed=2 * (count + width) * dim,
        ),
    )(rows, vocab, wanted.reshape(1, count), ids.reshape(width, 1))
    return tuple(o.reshape(count) for o in outs)


def on_device(hidden, norm_gain, unembed, targets, live):
    ny = lax.axis_size("y")
    nc = lax.axis_size("c")
    y = lax.axis_index("y")
    c = lax.axis_index("c")
    mine = hidden.shape[0]
    dim = hidden.shape[1]
    width = unembed.shape[0]

    wide = hidden.astype(jnp.float32)
    normed = (
        wide * lax.rsqrt(jnp.mean(wide * wide, axis=1, keepdims=True) + 1e-06) * norm_gain
    ).astype(jnp.bfloat16)

    code = jnp.zeros((mine, 16), jnp.bfloat16)
    code = code.at[:, 0].set((targets // 128).astype(jnp.bfloat16))
    code = code.at[:, 1].set((targets % 128).astype(jnp.bfloat16))
    block = jnp.concatenate([normed, code], axis=1)

    nx = lax.axis_size("x")
    x = lax.axis_index("x")
    block, unembed = lax.optimization_barrier((block, unembed))

    rings = {"y": (ny, block), "x": (nx, unembed)}
    got = {name: {0: start} for name, (size, start) in rings.items()}
    fronts = {name: {1: start, -1: start} for name, (size, start) in rings.items()}
    for step in range(1, ny // 2 + 1):
        moved = []
        for name, (size, start) in rings.items():
            for sign in (1, -1):
                reach = size // 2 if sign == 1 else size - 1 - size // 2
                if step <= reach:
                    fronts[name][sign] = shift(fronts[name][sign], name, size, sign)
                    got[name][(-sign * step) % size] = fronts[name][sign]
                    moved.append((name, sign))
        if step <= nx // 2:
            values = lax.optimization_barrier(tuple(fronts[n][s] for n, s in moved))
            for (n, s), v in zip(moved, values):
                fronts[n][s] = v
                got[n][(-s * step) % rings[n][0]] = v
    blocks = [got["y"][d] for d in range(ny)]
    near = [got["x"][d] for d in range(nx)]
    rows = jnp.concatenate([b[:, :dim] for b in blocks], axis=0)
    wanted = jnp.concatenate(
        [b[:, dim].astype(jnp.int32) * 128 + b[:, dim + 1].astype(jnp.int32) for b in blocks], axis=0
    )

    whole = lax.all_gather(jnp.concatenate(near, axis=0), ("z", "c"), axis=0, tiled=True)
    local = jnp.arange(whole.shape[0], dtype=jnp.int32)
    group, place = local // (nx * width), local % (nx * width)
    far_z, far_c = group // nc, group % nc
    far_x = (x + place // width) % nx
    ids = (((far_z * nx + far_x) * nc + far_c) * ny + y) * width + place % width

    stats = row_stats(rows, whole, wanted, ids)

    packed = jnp.roll(jnp.stack(stats).reshape(4, ny, mine), y, axis=1).reshape(4, ny * mine)
    got = lax.all_to_all(packed, "y", 1, 1, tiled=True).reshape(4, ny, mine)
    tops, totals, spreads, chosen = got[0], got[1], got[2], got[3]
    top = jnp.max(tops, axis=0)
    scale = jnp.exp(tops - top[None])
    total = jnp.sum(totals * scale, axis=0)
    spread = jnp.sum(scale * (spreads + (tops - top[None]) * totals), axis=0)
    picked = jnp.sum(chosen, axis=0)
    mask = live.astype(jnp.float32)
    logprob = (picked - top - jnp.log(total)) * mask
    entropy = (jnp.log(total) - spread / total) * mask
    return (logprob, entropy)


def solution(mesh):
    nz, nx, nc = 8, 4, 2
    ny = mesh.devices.shape[1]
    req = mesh.devices.shape[0]
    nz = req // (nx * nc)
    flat = Mesh(mesh.devices.reshape(nz, nx, nc, ny), FLAT)
    return jax.shard_map(
        on_device,
        mesh=flat,
        in_specs=(P(FLAT, None), P(), P(FLAT, None), P(FLAT), P(FLAT)),
        out_specs=(P(FLAT), P(FLAT)),
        check_vma=False,
    )
```

```python
import jax
import jax.numpy as jnp
from jax import lax
from jax.experimental import pallas as pl
from jax.sharding import Mesh, PartitionSpec as P

FLAT = ("z", "x", "c", "y")


def combine_stats(first, second):
    top = jnp.maximum(first[0], second[0])
    scale_one = jnp.exp(first[0] - top)
    scale_two = jnp.exp(second[0] - top)
    total = first[1] * scale_one + second[1] * scale_two
    spread = scale_one * (first[2] + (first[0] - top) * first[1]) + scale_two * (
        second[2] + (second[0] - top) * second[1]
    )
    return (top, total, spread, first[3] + second[3])


def shift(value, axis, size, step):
    return lax.ppermute(value, axis, [(i, (i + step) % size) for i in range(size)])


def chunk_stats(normed, piece, ids, wanted):
    logits = lax.dot_general(
        normed, piece, (((1,), (1,)), ((), ())), preferred_element_type=jnp.float32
    )
    chosen = jnp.sum(jnp.where(ids[None, :] == wanted[:, None], logits, 0.0), axis=1)
    fold_top = jnp.max(logits, axis=1)
    shifted = logits - fold_top[:, None]
    weights = jnp.exp(shifted)
    return (fold_top, jnp.sum(weights, axis=1), jnp.sum(weights * shifted, axis=1), chosen)


def stats_kernel(rows_ref, vocab_ref, wanted_ref, ids_ref, top_ref, total_ref, spread_ref, chosen_ref):
    j = pl.program_id(0)

    @pl.when(j == 0)
    def _():
        top_ref[...] = jnp.full(top_ref.shape, -1e30, jnp.float32)
        total_ref[...] = jnp.zeros(total_ref.shape, jnp.float32)
        spread_ref[...] = jnp.zeros(spread_ref.shape, jnp.float32)
        chosen_ref[...] = jnp.zeros(chosen_ref.shape, jnp.float32)

    logits = lax.dot_general(
        vocab_ref[...], rows_ref[...], (((1,), (1,)), ((), ())), preferred_element_type=jnp.float32
    )
    hit = ids_ref[...] == wanted_ref[...]
    chosen_ref[...] += jnp.sum(jnp.where(hit, logits, 0.0), axis=0, keepdims=True)
    fold = jnp.max(logits, axis=0, keepdims=True)
    shifted = logits - fold
    weights = jnp.exp(shifted)
    new_total = jnp.sum(weights, axis=0, keepdims=True)
    new_spread = jnp.sum(weights * shifted, axis=0, keepdims=True)
    old_top = top_ref[...]
    top = jnp.maximum(old_top, fold)
    scale_one = jnp.exp(old_top - top)
    scale_two = jnp.exp(fold - top)
    old_total = total_ref[...]
    total_ref[...] = old_total * scale_one + new_total * scale_two
    spread_ref[...] = scale_one * (spread_ref[...] + (old_top - top) * old_total) + scale_two * (
        new_spread + (fold - top) * new_total
    )
    top_ref[...] = top


def row_stats(rows, vocab, wanted, ids, tile=256):
    count, dim = rows.shape
    width = vocab.shape[0]
    line = pl.BlockSpec((1, count), lambda j: (0, 0))
    outs = pl.pallas_call(
        stats_kernel,
        grid=(width // tile,),
        in_specs=[
            pl.BlockSpec((count, dim), lambda j: (0, 0)),
            pl.BlockSpec((tile, dim), lambda j: (j, 0)),
            line,
            pl.BlockSpec((tile, 1), lambda j: (j, 0)),
        ],
        out_specs=[line, line, line, line],
        out_shape=[jax.ShapeDtypeStruct((1, count), jnp.float32)] * 4,
        cost_estimate=pl.CostEstimate(
            flops=2 * count * width * dim,
            transcendentals=count * width,
            bytes_accessed=2 * (count + width) * dim,
        ),
    )(rows, vocab, wanted.reshape(1, count), ids.reshape(width, 1))
    return tuple(o.reshape(count) for o in outs)


def on_device(hidden, norm_gain, unembed, targets, live):
    ny = lax.axis_size("y")
    nc = lax.axis_size("c")
    y = lax.axis_index("y")
    c = lax.axis_index("c")
    mine = hidden.shape[0]
    dim = hidden.shape[1]
    width = unembed.shape[0]

    wide = hidden.astype(jnp.float32)
    normed = (
        wide * lax.rsqrt(jnp.mean(wide * wide, axis=1, keepdims=True) + 1e-06) * norm_gain
    ).astype(jnp.bfloat16)

    code = jnp.zeros((mine, 16), jnp.bfloat16)
    code = code.at[:, 0].set((targets // 128).astype(jnp.bfloat16))
    code = code.at[:, 1].set((targets % 128).astype(jnp.bfloat16))
    block = jnp.concatenate([normed, code], axis=1)

    nx = lax.axis_size("x")
    x = lax.axis_index("x")
    block, unembed = lax.optimization_barrier((block, unembed))

    rings = {"y": (ny, block), "x": (nx, unembed)}
    got = {name: {0: start} for name, (size, start) in rings.items()}
    fronts = {name: {1: start, -1: start} for name, (size, start) in rings.items()}
    for step in range(1, ny // 2 + 1):
        moved = []
        for name, (size, start) in rings.items():
            for sign in (1, -1):
                reach = size // 2 if sign == 1 else size - 1 - size // 2
                if step <= reach:
                    fronts[name][sign] = shift(fronts[name][sign], name, size, sign)
                    got[name][(-sign * step) % size] = fronts[name][sign]
                    moved.append((name, sign))
        if step == 1:
            values = lax.optimization_barrier(tuple(fronts[n][s] for n, s in moved))
            for (n, s), v in zip(moved, values):
                fronts[n][s] = v
                got[n][(-s * step) % rings[n][0]] = v
    blocks = [got["y"][d] for d in range(ny)]
    near = [got["x"][d] for d in range(nx)]
    rows = jnp.concatenate([b[:, :dim] for b in blocks], axis=0)
    wanted = jnp.concatenate(
        [b[:, dim].astype(jnp.int32) * 128 + b[:, dim + 1].astype(jnp.int32) for b in blocks], axis=0
    )

    whole = lax.all_gather(jnp.concatenate(near, axis=0), ("z", "c"), axis=0, tiled=True)
    local = jnp.arange(whole.shape[0], dtype=jnp.int32)
    group, place = local // (nx * width), local % (nx * width)
    far_z, far_c = group // nc, group % nc
    far_x = (x + place // width) % nx
    ids = (((far_z * nx + far_x) * nc + far_c) * ny + y) * width + place % width

    stats = row_stats(rows, whole, wanted, ids)

    packed = jnp.roll(jnp.stack(stats).reshape(4, ny, mine), y, axis=1).reshape(4, ny * mine)
    got = lax.all_to_all(packed, "y", 1, 1, tiled=True).reshape(4, ny, mine)
    tops, totals, spreads, chosen = got[0], got[1], got[2], got[3]
    top = jnp.max(tops, axis=0)
    scale = jnp.exp(tops - top[None])
    total = jnp.sum(totals * scale, axis=0)
    spread = jnp.sum(scale * (spreads + (tops - top[None]) * totals), axis=0)
    picked = jnp.sum(chosen, axis=0)
    mask = live.astype(jnp.float32)
    logprob = (picked - top - jnp.log(total)) * mask
    entropy = (jnp.log(total) - spread / total) * mask
    return (logprob, entropy)


def solution(mesh):
    nz, nx, nc = 8, 4, 2
    ny = mesh.devices.shape[1]
    req = mesh.devices.shape[0]
    nz = req // (nx * nc)
    flat = Mesh(mesh.devices.reshape(nz, nx, nc, ny), FLAT)
    return jax.shard_map(
        on_device,
        mesh=flat,
        in_specs=(P(FLAT, None), P(), P(FLAT, None), P(FLAT), P(FLAT)),
        out_specs=(P(FLAT), P(FLAT)),
        check_vma=False,
    )
```

```python
import jax
import jax.numpy as jnp
from jax import lax
from jax.experimental import pallas as pl
from jax.sharding import Mesh, PartitionSpec as P

FLAT = ("z", "x", "c", "y")


def combine_stats(first, second):
    top = jnp.maximum(first[0], second[0])
    scale_one = jnp.exp(first[0] - top)
    scale_two = jnp.exp(second[0] - top)
    total = first[1] * scale_one + second[1] * scale_two
    spread = scale_one * (first[2] + (first[0] - top) * first[1]) + scale_two * (
        second[2] + (second[0] - top) * second[1]
    )
    return (top, total, spread, first[3] + second[3])


def shift(value, axis, size, step):
    return lax.ppermute(value, axis, [(i, (i + step) % size) for i in range(size)])


def chunk_stats(normed, piece, ids, wanted):
    logits = lax.dot_general(
        normed, piece, (((1,), (1,)), ((), ())), preferred_element_type=jnp.float32
    )
    chosen = jnp.sum(jnp.where(ids[None, :] == wanted[:, None], logits, 0.0), axis=1)
    fold_top = jnp.max(logits, axis=1)
    shifted = logits - fold_top[:, None]
    weights = jnp.exp(shifted)
    return (fold_top, jnp.sum(weights, axis=1), jnp.sum(weights * shifted, axis=1), chosen)


def stats_kernel(rows_ref, vocab_ref, wanted_ref, ids_ref, top_ref, total_ref, spread_ref, chosen_ref):
    j = pl.program_id(0)

    @pl.when(j == 0)
    def _():
        top_ref[...] = jnp.full(top_ref.shape, -1e30, jnp.float32)
        total_ref[...] = jnp.zeros(total_ref.shape, jnp.float32)
        spread_ref[...] = jnp.zeros(spread_ref.shape, jnp.float32)
        chosen_ref[...] = jnp.zeros(chosen_ref.shape, jnp.float32)

    logits = lax.dot_general(
        vocab_ref[...], rows_ref[...], (((1,), (1,)), ((), ())), preferred_element_type=jnp.float32
    )
    hit = ids_ref[...] == wanted_ref[...]
    chosen_ref[...] += jnp.sum(jnp.where(hit, logits, 0.0), axis=0, keepdims=True)
    fold = jnp.max(logits, axis=0, keepdims=True)
    shifted = logits - fold
    weights = jnp.exp(shifted)
    new_total = jnp.sum(weights, axis=0, keepdims=True)
    new_spread = jnp.sum(weights * shifted, axis=0, keepdims=True)
    old_top = top_ref[...]
    top = jnp.maximum(old_top, fold)
    scale_one = jnp.exp(old_top - top)
    scale_two = jnp.exp(fold - top)
    old_total = total_ref[...]
    total_ref[...] = old_total * scale_one + new_total * scale_two
    spread_ref[...] = scale_one * (spread_ref[...] + (old_top - top) * old_total) + scale_two * (
        new_spread + (fold - top) * new_total
    )
    top_ref[...] = top


def row_stats(rows, vocab, wanted, ids, tile=256):
    count, dim = rows.shape
    width = vocab.shape[0]
    line = pl.BlockSpec((1, count), lambda j: (0, 0))
    outs = pl.pallas_call(
        stats_kernel,
        grid=(width // tile,),
        in_specs=[
            pl.BlockSpec((count, dim), lambda j: (0, 0)),
            pl.BlockSpec((tile, dim), lambda j: (j, 0)),
            line,
            pl.BlockSpec((tile, 1), lambda j: (j, 0)),
        ],
        out_specs=[line, line, line, line],
        out_shape=[jax.ShapeDtypeStruct((1, count), jnp.float32)] * 4,
        cost_estimate=pl.CostEstimate(
            flops=2 * count * width * dim,
            transcendentals=count * width,
            bytes_accessed=2 * (count + width) * dim,
        ),
    )(rows, vocab, wanted.reshape(1, count), ids.reshape(width, 1))
    return tuple(o.reshape(count) for o in outs)


def on_device(hidden, norm_gain, unembed, targets, live):
    ny = lax.axis_size("y")
    nc = lax.axis_size("c")
    y = lax.axis_index("y")
    c = lax.axis_index("c")
    mine = hidden.shape[0]
    dim = hidden.shape[1]
    width = unembed.shape[0]

    wide = hidden.astype(jnp.float32)
    normed = (
        wide * lax.rsqrt(jnp.mean(wide * wide, axis=1, keepdims=True) + 1e-06) * norm_gain
    ).astype(jnp.bfloat16)

    code = jnp.zeros((mine, 16), jnp.bfloat16)
    code = code.at[:, 0].set((targets // 128).astype(jnp.bfloat16))
    code = code.at[:, 1].set((targets % 128).astype(jnp.bfloat16))
    block = jnp.concatenate([normed, code], axis=1)

    nx = lax.axis_size("x")
    x = lax.axis_index("x")
    near = [None] * nx
    near[0] = unembed
    fronts = {1: shift(unembed, "x", nx, 1), -1: shift(unembed, "x", nx, -1)}
    block, fronts[1], fronts[-1] = lax.optimization_barrier((block, fronts[1], fronts[-1]))
    for sign in (1, -1):
        cur = fronts[sign]
        reach = nx // 2 if sign == 1 else nx - 1 - nx // 2
        for step in range(1, reach + 1):
            if step > 1:
                cur = shift(cur, "x", nx, sign)
            near[(-sign * step) % nx] = cur

    blocks = [None] * ny
    blocks[0] = block
    for sign in (1, -1):
        cur = block
        reach = ny // 2 if sign == 1 else ny - 1 - ny // 2
        for step in range(1, reach + 1):
            cur = shift(cur, "y", ny, sign)
            blocks[(-sign * step) % ny] = cur
    rows = jnp.concatenate([b[:, :dim] for b in blocks], axis=0)
    wanted = jnp.concatenate(
        [b[:, dim].astype(jnp.int32) * 128 + b[:, dim + 1].astype(jnp.int32) for b in blocks], axis=0
    )

    whole = lax.all_gather(jnp.concatenate(near, axis=0), ("z", "c"), axis=0, tiled=True)
    local = jnp.arange(whole.shape[0], dtype=jnp.int32)
    group, place = local // (nx * width), local % (nx * width)
    far_z, far_c = group // nc, group % nc
    far_x = (x + place // width) % nx
    ids = (((far_z * nx + far_x) * nc + far_c) * ny + y) * width + place % width

    stats = row_stats(rows, whole, wanted, ids)

    packed = jnp.roll(jnp.stack(stats).reshape(4, ny, mine), y, axis=1).reshape(4, ny * mine)
    got = lax.all_to_all(packed, "y", 1, 1, tiled=True).reshape(4, ny, mine)
    tops, totals, spreads, chosen = got[0], got[1], got[2], got[3]
    top = jnp.max(tops, axis=0)
    scale = jnp.exp(tops - top[None])
    total = jnp.sum(totals * scale, axis=0)
    spread = jnp.sum(scale * (spreads + (tops - top[None]) * totals), axis=0)
    picked = jnp.sum(chosen, axis=0)
    mask = live.astype(jnp.float32)
    logprob = (picked - top - jnp.log(total)) * mask
    entropy = (jnp.log(total) - spread / total) * mask
    return (logprob, entropy)


def solution(mesh):
    nz, nx, nc = 8, 4, 2
    ny = mesh.devices.shape[1]
    req = mesh.devices.shape[0]
    nz = req // (nx * nc)
    flat = Mesh(mesh.devices.reshape(nz, nx, nc, ny), FLAT)
    return jax.shard_map(
        on_device,
        mesh=flat,
        in_specs=(P(FLAT, None), P(), P(FLAT, None), P(FLAT), P(FLAT)),
        out_specs=(P(FLAT), P(FLAT)),
        check_vma=False,
    )
```

```python
import jax
import jax.numpy as jnp
from jax import lax
from jax.experimental import pallas as pl
from jax.sharding import Mesh, PartitionSpec as P

FLAT = ("z", "x", "c", "y")


def combine_stats(first, second):
    top = jnp.maximum(first[0], second[0])
    scale_one = jnp.exp(first[0] - top)
    scale_two = jnp.exp(second[0] - top)
    total = first[1] * scale_one + second[1] * scale_two
    spread = scale_one * (first[2] + (first[0] - top) * first[1]) + scale_two * (
        second[2] + (second[0] - top) * second[1]
    )
    return (top, total, spread, first[3] + second[3])


def shift(value, axis, size, step):
    return lax.ppermute(value, axis, [(i, (i + step) % size) for i in range(size)])


def chunk_stats(normed, piece, ids, wanted):
    logits = lax.dot_general(
        normed, piece, (((1,), (1,)), ((), ())), preferred_element_type=jnp.float32
    )
    chosen = jnp.sum(jnp.where(ids[None, :] == wanted[:, None], logits, 0.0), axis=1)
    fold_top = jnp.max(logits, axis=1)
    shifted = logits - fold_top[:, None]
    weights = jnp.exp(shifted)
    return (fold_top, jnp.sum(weights, axis=1), jnp.sum(weights * shifted, axis=1), chosen)


def stats_kernel(rows_ref, vocab_ref, wanted_ref, ids_ref, top_ref, total_ref, spread_ref, chosen_ref):
    j = pl.program_id(0)

    @pl.when(j == 0)
    def _():
        top_ref[...] = jnp.full(top_ref.shape, -1e30, jnp.float32)
        total_ref[...] = jnp.zeros(total_ref.shape, jnp.float32)
        spread_ref[...] = jnp.zeros(spread_ref.shape, jnp.float32)
        chosen_ref[...] = jnp.zeros(chosen_ref.shape, jnp.float32)

    logits = lax.dot_general(
        vocab_ref[...], rows_ref[...], (((1,), (1,)), ((), ())), preferred_element_type=jnp.float32
    )
    hit = ids_ref[...] == wanted_ref[...]
    chosen_ref[...] += jnp.sum(jnp.where(hit, logits, 0.0), axis=0, keepdims=True)
    fold = jnp.max(logits, axis=0, keepdims=True)
    shifted = logits - fold
    weights = jnp.exp(shifted)
    new_total = jnp.sum(weights, axis=0, keepdims=True)
    new_spread = jnp.sum(weights * shifted, axis=0, keepdims=True)
    old_top = top_ref[...]
    top = jnp.maximum(old_top, fold)
    scale_one = jnp.exp(old_top - top)
    scale_two = jnp.exp(fold - top)
    old_total = total_ref[...]
    total_ref[...] = old_total * scale_one + new_total * scale_two
    spread_ref[...] = scale_one * (spread_ref[...] + (old_top - top) * old_total) + scale_two * (
        new_spread + (fold - top) * new_total
    )
    top_ref[...] = top


def row_stats(rows, vocab, wanted, ids, tile=256):
    count, dim = rows.shape
    width = vocab.shape[0]
    line = pl.BlockSpec((1, count), lambda j: (0, 0))
    outs = pl.pallas_call(
        stats_kernel,
        grid=(width // tile,),
        in_specs=[
            pl.BlockSpec((count, dim), lambda j: (0, 0)),
            pl.BlockSpec((tile, dim), lambda j: (j, 0)),
            line,
            pl.BlockSpec((tile, 1), lambda j: (j, 0)),
        ],
        out_specs=[line, line, line, line],
        out_shape=[jax.ShapeDtypeStruct((1, count), jnp.float32)] * 4,
        cost_estimate=pl.CostEstimate(
            flops=2 * count * width * dim,
            transcendentals=count * width,
            bytes_accessed=2 * (count + width) * dim,
        ),
    )(rows, vocab, wanted.reshape(1, count), ids.reshape(width, 1))
    return tuple(o.reshape(count) for o in outs)


def on_device(hidden, norm_gain, unembed, targets, live):
    ny = lax.axis_size("y")
    nc = lax.axis_size("c")
    y = lax.axis_index("y")
    c = lax.axis_index("c")
    mine = hidden.shape[0]
    dim = hidden.shape[1]
    width = unembed.shape[0]

    wide = hidden.astype(jnp.float32)
    normed = (
        wide * lax.rsqrt(jnp.mean(wide * wide, axis=1, keepdims=True) + 1e-06) * norm_gain
    ).astype(jnp.bfloat16)

    code = jnp.zeros((mine, 16), jnp.bfloat16)
    code = code.at[:, 0].set((targets // 128).astype(jnp.bfloat16))
    code = code.at[:, 1].set((targets % 128).astype(jnp.bfloat16))
    block = jnp.concatenate([normed, code], axis=1)

    nx = lax.axis_size("x")
    x = lax.axis_index("x")
    near = [unembed] + [shift(unembed, "x", nx, -d) for d in range(1, nx)]
    block, *rest = lax.optimization_barrier((block, *near[1:]))
    near[1:] = rest

    blocks = [None] * ny
    blocks[0] = block
    for sign in (1, -1):
        cur = block
        reach = ny // 2 if sign == 1 else ny - 1 - ny // 2
        for step in range(1, reach + 1):
            cur = shift(cur, "y", ny, sign)
            blocks[(-sign * step) % ny] = cur
    rows = jnp.concatenate([b[:, :dim] for b in blocks], axis=0)
    wanted = jnp.concatenate(
        [b[:, dim].astype(jnp.int32) * 128 + b[:, dim + 1].astype(jnp.int32) for b in blocks], axis=0
    )

    whole = lax.all_gather(jnp.concatenate(near, axis=0), ("z", "c"), axis=0, tiled=True)
    local = jnp.arange(whole.shape[0], dtype=jnp.int32)
    group, place = local // (nx * width), local % (nx * width)
    far_z, far_c = group // nc, group % nc
    far_x = (x + place // width) % nx
    ids = (((far_z * nx + far_x) * nc + far_c) * ny + y) * width + place % width

    stats = row_stats(rows, whole, wanted, ids)

    packed = jnp.roll(jnp.stack(stats).reshape(4, ny, mine), y, axis=1).reshape(4, ny * mine)
    got = lax.all_to_all(packed, "y", 1, 1, tiled=True).reshape(4, ny, mine)
    tops, totals, spreads, chosen = got[0], got[1], got[2], got[3]
    top = jnp.max(tops, axis=0)
    scale = jnp.exp(tops - top[None])
    total = jnp.sum(totals * scale, axis=0)
    spread = jnp.sum(scale * (spreads + (tops - top[None]) * totals), axis=0)
    picked = jnp.sum(chosen, axis=0)
    mask = live.astype(jnp.float32)
    logprob = (picked - top - jnp.log(total)) * mask
    entropy = (jnp.log(total) - spread / total) * mask
    return (logprob, entropy)


def solution(mesh):
    nz, nx, nc = 8, 4, 2
    ny = mesh.devices.shape[1]
    req = mesh.devices.shape[0]
    nz = req // (nx * nc)
    flat = Mesh(mesh.devices.reshape(nz, nx, nc, ny), FLAT)
    return jax.shard_map(
        on_device,
        mesh=flat,
        in_specs=(P(FLAT, None), P(), P(FLAT, None), P(FLAT), P(FLAT)),
        out_specs=(P(FLAT), P(FLAT)),
        check_vma=False,
    )
```

```python
import jax
import jax.numpy as jnp
from jax import lax
from jax.experimental import pallas as pl
from jax.sharding import Mesh, PartitionSpec as P

FLAT = ("z", "x", "c", "y")


def combine_stats(first, second):
    top = jnp.maximum(first[0], second[0])
    scale_one = jnp.exp(first[0] - top)
    scale_two = jnp.exp(second[0] - top)
    total = first[1] * scale_one + second[1] * scale_two
    spread = scale_one * (first[2] + (first[0] - top) * first[1]) + scale_two * (
        second[2] + (second[0] - top) * second[1]
    )
    return (top, total, spread, first[3] + second[3])


def shift(value, axis, size, step):
    return lax.ppermute(value, axis, [(i, (i + step) % size) for i in range(size)])


def chunk_stats(normed, piece, ids, wanted):
    logits = lax.dot_general(
        normed, piece, (((1,), (1,)), ((), ())), preferred_element_type=jnp.float32
    )
    chosen = jnp.sum(jnp.where(ids[None, :] == wanted[:, None], logits, 0.0), axis=1)
    fold_top = jnp.max(logits, axis=1)
    shifted = logits - fold_top[:, None]
    weights = jnp.exp(shifted)
    return (fold_top, jnp.sum(weights, axis=1), jnp.sum(weights * shifted, axis=1), chosen)


def stats_kernel(rows_ref, vocab_ref, wanted_ref, ids_ref, top_ref, total_ref, spread_ref, chosen_ref):
    j = pl.program_id(0)

    @pl.when(j == 0)
    def _():
        top_ref[...] = jnp.full(top_ref.shape, -1e30, jnp.float32)
        total_ref[...] = jnp.zeros(total_ref.shape, jnp.float32)
        spread_ref[...] = jnp.zeros(spread_ref.shape, jnp.float32)
        chosen_ref[...] = jnp.zeros(chosen_ref.shape, jnp.float32)

    logits = lax.dot_general(
        vocab_ref[...], rows_ref[...], (((1,), (1,)), ((), ())), preferred_element_type=jnp.float32
    )
    hit = ids_ref[...] == wanted_ref[...]
    chosen_ref[...] += jnp.sum(jnp.where(hit, logits, 0.0), axis=0, keepdims=True)
    fold = jnp.max(logits, axis=0, keepdims=True)
    shifted = logits - fold
    weights = jnp.exp(shifted)
    new_total = jnp.sum(weights, axis=0, keepdims=True)
    new_spread = jnp.sum(weights * shifted, axis=0, keepdims=True)
    old_top = top_ref[...]
    top = jnp.maximum(old_top, fold)
    scale_one = jnp.exp(old_top - top)
    scale_two = jnp.exp(fold - top)
    old_total = total_ref[...]
    total_ref[...] = old_total * scale_one + new_total * scale_two
    spread_ref[...] = scale_one * (spread_ref[...] + (old_top - top) * old_total) + scale_two * (
        new_spread + (fold - top) * new_total
    )
    top_ref[...] = top


def row_stats(rows, vocab, wanted, ids, tile=512):
    count, dim = rows.shape
    width = vocab.shape[0]
    line = pl.BlockSpec((1, count), lambda j: (0, 0))
    outs = pl.pallas_call(
        stats_kernel,
        grid=(width // tile,),
        in_specs=[
            pl.BlockSpec((count, dim), lambda j: (0, 0)),
            pl.BlockSpec((tile, dim), lambda j: (j, 0)),
            line,
            pl.BlockSpec((tile, 1), lambda j: (j, 0)),
        ],
        out_specs=[line, line, line, line],
        out_shape=[jax.ShapeDtypeStruct((1, count), jnp.float32)] * 4,
        cost_estimate=pl.CostEstimate(
            flops=2 * count * width * dim,
            transcendentals=count * width,
            bytes_accessed=2 * (count + width) * dim,
        ),
    )(rows, vocab, wanted.reshape(1, count), ids.reshape(width, 1))
    return tuple(o.reshape(count) for o in outs)


def on_device(hidden, norm_gain, unembed, targets, live):
    ny = lax.axis_size("y")
    nc = lax.axis_size("c")
    y = lax.axis_index("y")
    c = lax.axis_index("c")
    mine = hidden.shape[0]
    dim = hidden.shape[1]
    width = unembed.shape[0]

    wide = hidden.astype(jnp.float32)
    normed = (
        wide * lax.rsqrt(jnp.mean(wide * wide, axis=1, keepdims=True) + 1e-06) * norm_gain
    ).astype(jnp.bfloat16)

    code = jnp.zeros((mine, 16), jnp.bfloat16)
    code = code.at[:, 0].set((targets // 128).astype(jnp.bfloat16))
    code = code.at[:, 1].set((targets % 128).astype(jnp.bfloat16))
    block = jnp.concatenate([normed, code], axis=1)

    nx = lax.axis_size("x")
    x = lax.axis_index("x")
    block, unembed = lax.optimization_barrier((block, unembed))
    near = [unembed] + [shift(unembed, "x", nx, -d) for d in range(1, nx)]

    blocks = [None] * ny
    blocks[0] = block
    for sign in (1, -1):
        cur = block
        reach = ny // 2 if sign == 1 else ny - 1 - ny // 2
        for step in range(1, reach + 1):
            cur = shift(cur, "y", ny, sign)
            blocks[(-sign * step) % ny] = cur
    rows = jnp.concatenate([b[:, :dim] for b in blocks], axis=0)
    wanted = jnp.concatenate(
        [b[:, dim].astype(jnp.int32) * 128 + b[:, dim + 1].astype(jnp.int32) for b in blocks], axis=0
    )

    whole = lax.all_gather(jnp.concatenate(near, axis=0), ("z", "c"), axis=0, tiled=True)
    local = jnp.arange(whole.shape[0], dtype=jnp.int32)
    group, place = local // (nx * width), local % (nx * width)
    far_z, far_c = group // nc, group % nc
    far_x = (x + place // width) % nx
    ids = (((far_z * nx + far_x) * nc + far_c) * ny + y) * width + place % width

    stats = row_stats(rows, whole, wanted, ids)

    packed = jnp.roll(jnp.stack(stats).reshape(4, ny, mine), y, axis=1).reshape(4, ny * mine)
    got = lax.all_to_all(packed, "y", 1, 1, tiled=True).reshape(4, ny, mine)
    tops, totals, spreads, chosen = got[0], got[1], got[2], got[3]
    top = jnp.max(tops, axis=0)
    scale = jnp.exp(tops - top[None])
    total = jnp.sum(totals * scale, axis=0)
    spread = jnp.sum(scale * (spreads + (tops - top[None]) * totals), axis=0)
    picked = jnp.sum(chosen, axis=0)
    mask = live.astype(jnp.float32)
    logprob = (picked - top - jnp.log(total)) * mask
    entropy = (jnp.log(total) - spread / total) * mask
    return (logprob, entropy)


def solution(mesh):
    nz, nx, nc = 8, 4, 2
    ny = mesh.devices.shape[1]
    req = mesh.devices.shape[0]
    nz = req // (nx * nc)
    flat = Mesh(mesh.devices.reshape(nz, nx, nc, ny), FLAT)
    return jax.shard_map(
        on_device,
        mesh=flat,
        in_specs=(P(FLAT, None), P(), P(FLAT, None), P(FLAT), P(FLAT)),
        out_specs=(P(FLAT), P(FLAT)),
        check_vma=False,
    )
```

```python
import functools

import jax
import jax.numpy as jnp
from jax import lax
from jax.experimental import pallas as pl
from jax.experimental.pallas import tpu as pltpu
from jax.sharding import Mesh, PartitionSpec as P

FLAT = ("z", "x", "c", "y")


def combine_stats(first, second):
    top = jnp.maximum(first[0], second[0])
    scale_one = jnp.exp(first[0] - top)
    scale_two = jnp.exp(second[0] - top)
    total = first[1] * scale_one + second[1] * scale_two
    spread = scale_one * (first[2] + (first[0] - top) * first[1]) + scale_two * (
        second[2] + (second[0] - top) * second[1]
    )
    return (top, total, spread, first[3] + second[3])


def shift(value, axis, size, step):
    return lax.ppermute(value, axis, [(i, (i + step) % size) for i in range(size)])


def chunk_stats(normed, piece, ids, wanted):
    logits = lax.dot_general(
        normed, piece, (((1,), (1,)), ((), ())), preferred_element_type=jnp.float32
    )
    chosen = jnp.sum(jnp.where(ids[None, :] == wanted[:, None], logits, 0.0), axis=1)
    fold_top = jnp.max(logits, axis=1)
    shifted = logits - fold_top[:, None]
    weights = jnp.exp(shifted)
    return (fold_top, jnp.sum(weights, axis=1), jnp.sum(weights * shifted, axis=1), chosen)


def stats_kernel(
    sizes, where_ref, rows_ref, vocab_ref, wanted_ref, top_ref, total_ref, spread_ref, chosen_ref
):
    j = pl.program_id(0)
    nx, nc, ny, width = sizes
    tile = vocab_ref.shape[0]
    x, y = where_ref[0], where_ref[1]
    local = j * tile + lax.broadcasted_iota(jnp.int32, (tile, 1), 0)
    group, place = local // (nx * width), local % (nx * width)
    far_x = (x + place // width) % nx
    ids = ((((group // nc) * nx + far_x) * nc + group % nc) * ny + y) * width + place % width

    @pl.when(j == 0)
    def _():
        top_ref[...] = jnp.full(top_ref.shape, -1e30, jnp.float32)
        total_ref[...] = jnp.zeros(total_ref.shape, jnp.float32)
        spread_ref[...] = jnp.zeros(spread_ref.shape, jnp.float32)
        chosen_ref[...] = jnp.zeros(chosen_ref.shape, jnp.float32)

    logits = lax.dot_general(
        vocab_ref[...], rows_ref[...], (((1,), (1,)), ((), ())), preferred_element_type=jnp.float32
    )
    hit = ids == wanted_ref[...]
    chosen_ref[...] += jnp.sum(jnp.where(hit, logits, 0.0), axis=0, keepdims=True)
    fold = jnp.max(logits, axis=0, keepdims=True)
    shifted = logits - fold
    weights = jnp.exp(shifted)
    new_total = jnp.sum(weights, axis=0, keepdims=True)
    new_spread = jnp.sum(weights * shifted, axis=0, keepdims=True)
    old_top = top_ref[...]
    top = jnp.maximum(old_top, fold)
    scale_one = jnp.exp(old_top - top)
    scale_two = jnp.exp(fold - top)
    old_total = total_ref[...]
    total_ref[...] = old_total * scale_one + new_total * scale_two
    spread_ref[...] = scale_one * (spread_ref[...] + (old_top - top) * old_total) + scale_two * (
        new_spread + (fold - top) * new_total
    )
    top_ref[...] = top


def row_stats(rows, vocab, wanted, where, sizes, tile=512):
    count, dim = rows.shape
    width = vocab.shape[0]
    line = pl.BlockSpec((1, count), lambda j: (0, 0))
    outs = pl.pallas_call(
        functools.partial(stats_kernel, sizes),
        grid=(width // tile,),
        in_specs=[
            pl.BlockSpec(memory_space=pltpu.SMEM),
            pl.BlockSpec((count, dim), lambda j: (0, 0)),
            pl.BlockSpec((tile, dim), lambda j: (j, 0)),
            line,
        ],
        out_specs=[line, line, line, line],
        out_shape=[jax.ShapeDtypeStruct((1, count), jnp.float32)] * 4,
        cost_estimate=pl.CostEstimate(
            flops=2 * count * width * dim,
            transcendentals=count * width,
            bytes_accessed=2 * (count + width) * dim,
        ),
    )(where, rows, vocab, wanted.reshape(1, count))
    return tuple(o.reshape(count) for o in outs)


def on_device(hidden, norm_gain, unembed, targets, live):
    ny = lax.axis_size("y")
    nc = lax.axis_size("c")
    y = lax.axis_index("y")
    c = lax.axis_index("c")
    mine = hidden.shape[0]
    dim = hidden.shape[1]
    width = unembed.shape[0]

    wide = hidden.astype(jnp.float32)
    normed = (
        wide * lax.rsqrt(jnp.mean(wide * wide, axis=1, keepdims=True) + 1e-06) * norm_gain
    ).astype(jnp.bfloat16)

    code = jnp.zeros((mine, 16), jnp.bfloat16)
    code = code.at[:, 0].set((targets // 128).astype(jnp.bfloat16))
    code = code.at[:, 1].set((targets % 128).astype(jnp.bfloat16))
    block = jnp.concatenate([normed, code], axis=1)

    nx = lax.axis_size("x")
    x = lax.axis_index("x")
    near = [unembed] + [shift(unembed, "x", nx, -d) for d in range(1, nx)]
    block, *rest = lax.optimization_barrier((block, *near[1:]))
    near[1:] = rest

    blocks = [None] * ny
    blocks[0] = block
    for sign in (1, -1):
        cur = block
        reach = ny // 2 if sign == 1 else ny - 1 - ny // 2
        for step in range(1, reach + 1):
            cur = shift(cur, "y", ny, sign)
            blocks[(-sign * step) % ny] = cur
    rows = jnp.concatenate([b[:, :dim] for b in blocks], axis=0)
    wanted = jnp.concatenate(
        [b[:, dim].astype(jnp.int32) * 128 + b[:, dim + 1].astype(jnp.int32) for b in blocks], axis=0
    )

    whole = lax.all_gather(jnp.concatenate(near, axis=0), ("z", "c"), axis=0, tiled=True)
    where = jnp.stack([x, y]).astype(jnp.int32)
    stats = row_stats(rows, whole, wanted, where, (nx, nc, ny, width))

    packed = jnp.roll(jnp.stack(stats).reshape(4, ny, mine), y, axis=1).reshape(4, ny * mine)
    got = lax.all_to_all(packed, "y", 1, 1, tiled=True).reshape(4, ny, mine)
    tops, totals, spreads, chosen = got[0], got[1], got[2], got[3]
    top = jnp.max(tops, axis=0)
    scale = jnp.exp(tops - top[None])
    total = jnp.sum(totals * scale, axis=0)
    spread = jnp.sum(scale * (spreads + (tops - top[None]) * totals), axis=0)
    picked = jnp.sum(chosen, axis=0)
    mask = live.astype(jnp.float32)
    logprob = (picked - top - jnp.log(total)) * mask
    entropy = (jnp.log(total) - spread / total) * mask
    return (logprob, entropy)


def solution(mesh):
    nz, nx, nc = 8, 4, 2
    ny = mesh.devices.shape[1]
    req = mesh.devices.shape[0]
    nz = req // (nx * nc)
    flat = Mesh(mesh.devices.reshape(nz, nx, nc, ny), FLAT)
    return jax.shard_map(
        on_device,
        mesh=flat,
        in_specs=(P(FLAT, None), P(), P(FLAT, None), P(FLAT), P(FLAT)),
        out_specs=(P(FLAT), P(FLAT)),
        check_vma=False,
    )
```

```python
import jax
import jax.numpy as jnp
from jax import lax
from jax.experimental import pallas as pl
from jax.sharding import Mesh, PartitionSpec as P

FLAT = ("z", "x", "c", "y")


def combine_stats(first, second):
    top = jnp.maximum(first[0], second[0])
    scale_one = jnp.exp(first[0] - top)
    scale_two = jnp.exp(second[0] - top)
    total = first[1] * scale_one + second[1] * scale_two
    spread = scale_one * (first[2] + (first[0] - top) * first[1]) + scale_two * (
        second[2] + (second[0] - top) * second[1]
    )
    return (top, total, spread, first[3] + second[3])


def shift(value, axis, size, step):
    return lax.ppermute(value, axis, [(i, (i + step) % size) for i in range(size)])


def chunk_stats(normed, piece, ids, wanted):
    logits = lax.dot_general(
        normed, piece, (((1,), (1,)), ((), ())), preferred_element_type=jnp.float32
    )
    chosen = jnp.sum(jnp.where(ids[None, :] == wanted[:, None], logits, 0.0), axis=1)
    fold_top = jnp.max(logits, axis=1)
    shifted = logits - fold_top[:, None]
    weights = jnp.exp(shifted)
    return (fold_top, jnp.sum(weights, axis=1), jnp.sum(weights * shifted, axis=1), chosen)


def stats_kernel(rows_ref, vocab_ref, spot_ref, top_ref, total_ref, spread_ref, chosen_ref):
    j = pl.program_id(0)
    tile = vocab_ref.shape[0]
    position = j * tile + lax.broadcasted_iota(jnp.int32, (tile, 1), 0)

    @pl.when(j == 0)
    def _():
        top_ref[...] = jnp.full(top_ref.shape, -1e30, jnp.float32)
        total_ref[...] = jnp.zeros(total_ref.shape, jnp.float32)
        spread_ref[...] = jnp.zeros(spread_ref.shape, jnp.float32)
        chosen_ref[...] = jnp.zeros(chosen_ref.shape, jnp.float32)

    logits = lax.dot_general(
        vocab_ref[...], rows_ref[...], (((1,), (1,)), ((), ())), preferred_element_type=jnp.float32
    )
    hit = position == spot_ref[...]
    chosen_ref[...] += jnp.sum(jnp.where(hit, logits, 0.0), axis=0, keepdims=True)
    fold = jnp.max(logits, axis=0, keepdims=True)
    shifted = logits - fold
    weights = jnp.exp(shifted)
    new_total = jnp.sum(weights, axis=0, keepdims=True)
    new_spread = jnp.sum(weights * shifted, axis=0, keepdims=True)
    old_top = top_ref[...]
    top = jnp.maximum(old_top, fold)
    scale_one = jnp.exp(old_top - top)
    scale_two = jnp.exp(fold - top)
    old_total = total_ref[...]
    total_ref[...] = old_total * scale_one + new_total * scale_two
    spread_ref[...] = scale_one * (spread_ref[...] + (old_top - top) * old_total) + scale_two * (
        new_spread + (fold - top) * new_total
    )
    top_ref[...] = top


def row_stats(rows, vocab, spot, tile=512):
    count, dim = rows.shape
    width = vocab.shape[0]
    line = pl.BlockSpec((1, count), lambda j: (0, 0))
    outs = pl.pallas_call(
        stats_kernel,
        grid=(width // tile,),
        in_specs=[
            pl.BlockSpec((count, dim), lambda j: (0, 0)),
            pl.BlockSpec((tile, dim), lambda j: (j, 0)),
            line,
        ],
        out_specs=[line, line, line, line],
        out_shape=[jax.ShapeDtypeStruct((1, count), jnp.float32)] * 4,
        cost_estimate=pl.CostEstimate(
            flops=2 * count * width * dim,
            transcendentals=count * width,
            bytes_accessed=2 * (count + width) * dim,
        ),
    )(rows, vocab, spot.reshape(1, count))
    return tuple(o.reshape(count) for o in outs)


def on_device(hidden, norm_gain, unembed, targets, live):
    ny = lax.axis_size("y")
    nc = lax.axis_size("c")
    y = lax.axis_index("y")
    c = lax.axis_index("c")
    mine = hidden.shape[0]
    dim = hidden.shape[1]
    width = unembed.shape[0]

    wide = hidden.astype(jnp.float32)
    normed = (
        wide * lax.rsqrt(jnp.mean(wide * wide, axis=1, keepdims=True) + 1e-06) * norm_gain
    ).astype(jnp.bfloat16)

    code = jnp.zeros((mine, 16), jnp.bfloat16)
    code = code.at[:, 0].set((targets // 128).astype(jnp.bfloat16))
    code = code.at[:, 1].set((targets % 128).astype(jnp.bfloat16))
    block = jnp.concatenate([normed, code], axis=1)

    nx = lax.axis_size("x")
    x = lax.axis_index("x")
    near = [unembed] + [shift(unembed, "x", nx, -d) for d in range(1, nx)]
    block, *rest = lax.optimization_barrier((block, *near[1:]))
    near[1:] = rest

    blocks = [None] * ny
    blocks[0] = block
    for sign in (1, -1):
        cur = block
        reach = ny // 2 if sign == 1 else ny - 1 - ny // 2
        for step in range(1, reach + 1):
            cur = shift(cur, "y", ny, sign)
            blocks[(-sign * step) % ny] = cur
    rows = jnp.concatenate([b[:, :dim] for b in blocks], axis=0)
    wanted = jnp.concatenate(
        [b[:, dim].astype(jnp.int32) * 128 + b[:, dim + 1].astype(jnp.int32) for b in blocks], axis=0
    )

    whole = lax.all_gather(jnp.concatenate(near, axis=0), ("z", "c"), axis=0, tiled=True)
    owner, entry = wanted // width, wanted % width
    req, shard = owner // ny, owner % ny
    far_c, far_x, far_z = req % nc, (req // nc) % nx, req // (nc * nx)
    spot = ((far_z * nc + far_c) * nx + (far_x - x) % nx) * width + entry
    spot = jnp.where(shard == y, spot, -1)

    stats = row_stats(rows, whole, spot)

    packed = jnp.roll(jnp.stack(stats).reshape(4, ny, mine), y, axis=1).reshape(4, ny * mine)
    got = lax.all_to_all(packed, "y", 1, 1, tiled=True).reshape(4, ny, mine)
    tops, totals, spreads, chosen = got[0], got[1], got[2], got[3]
    top = jnp.max(tops, axis=0)
    scale = jnp.exp(tops - top[None])
    total = jnp.sum(totals * scale, axis=0)
    spread = jnp.sum(scale * (spreads + (tops - top[None]) * totals), axis=0)
    picked = jnp.sum(chosen, axis=0)
    mask = live.astype(jnp.float32)
    logprob = (picked - top - jnp.log(total)) * mask
    entropy = (jnp.log(total) - spread / total) * mask
    return (logprob, entropy)


def solution(mesh):
    nz, nx, nc = 8, 4, 2
    ny = mesh.devices.shape[1]
    req = mesh.devices.shape[0]
    nz = req // (nx * nc)
    flat = Mesh(mesh.devices.reshape(nz, nx, nc, ny), FLAT)
    return jax.shard_map(
        on_device,
        mesh=flat,
        in_specs=(P(FLAT, None), P(), P(FLAT, None), P(FLAT), P(FLAT)),
        out_specs=(P(FLAT), P(FLAT)),
        check_vma=False,
    )
```

```python
import jax
import jax.numpy as jnp
from jax import lax
from jax.experimental import pallas as pl
from jax.sharding import Mesh, PartitionSpec as P

FLAT = ("z", "x", "c", "y")


def combine_stats(first, second):
    top = jnp.maximum(first[0], second[0])
    scale_one = jnp.exp(first[0] - top)
    scale_two = jnp.exp(second[0] - top)
    total = first[1] * scale_one + second[1] * scale_two
    spread = scale_one * (first[2] + (first[0] - top) * first[1]) + scale_two * (
        second[2] + (second[0] - top) * second[1]
    )
    return (top, total, spread, first[3] + second[3])


def shift(value, axis, size, step):
    return lax.ppermute(value, axis, [(i, (i + step) % size) for i in range(size)])


def chunk_stats(normed, piece, ids, wanted):
    logits = lax.dot_general(
        normed, piece, (((1,), (1,)), ((), ())), preferred_element_type=jnp.float32
    )
    chosen = jnp.sum(jnp.where(ids[None, :] == wanted[:, None], logits, 0.0), axis=1)
    fold_top = jnp.max(logits, axis=1)
    shifted = logits - fold_top[:, None]
    weights = jnp.exp(shifted)
    return (fold_top, jnp.sum(weights, axis=1), jnp.sum(weights * shifted, axis=1), chosen)


def stats_kernel(rows_ref, vocab_ref, spot_ref, top_ref, total_ref, spread_ref, chosen_ref):
    j = pl.program_id(0)
    tile = vocab_ref.shape[0]
    position = j * tile + lax.broadcasted_iota(jnp.int32, (tile, 1), 0)

    @pl.when(j == 0)
    def _():
        top_ref[...] = jnp.full(top_ref.shape, -1e30, jnp.float32)
        total_ref[...] = jnp.zeros(total_ref.shape, jnp.float32)
        spread_ref[...] = jnp.zeros(spread_ref.shape, jnp.float32)
        chosen_ref[...] = jnp.zeros(chosen_ref.shape, jnp.float32)

    logits = lax.dot_general(
        vocab_ref[...], rows_ref[...], (((1,), (1,)), ((), ())), preferred_element_type=jnp.float32
    )
    hit = position == spot_ref[...]
    chosen_ref[...] += jnp.sum(jnp.where(hit, logits, 0.0), axis=0, keepdims=True)
    fold = jnp.max(logits, axis=0, keepdims=True)
    shifted = logits - fold
    weights = jnp.exp(shifted)
    new_total = jnp.sum(weights, axis=0, keepdims=True)
    new_spread = jnp.sum(weights * shifted, axis=0, keepdims=True)
    old_top = top_ref[...]
    top = jnp.maximum(old_top, fold)
    scale_one = jnp.exp(old_top - top)
    scale_two = jnp.exp(fold - top)
    old_total = total_ref[...]
    total_ref[...] = old_total * scale_one + new_total * scale_two
    spread_ref[...] = scale_one * (spread_ref[...] + (old_top - top) * old_total) + scale_two * (
        new_spread + (fold - top) * new_total
    )
    top_ref[...] = top


def row_stats(rows, vocab, spot, tile=512):
    count, dim = rows.shape
    width = vocab.shape[0]
    line = pl.BlockSpec((1, count), lambda j: (0, 0))
    outs = pl.pallas_call(
        stats_kernel,
        grid=(width // tile,),
        in_specs=[
            pl.BlockSpec((count, dim), lambda j: (0, 0)),
            pl.BlockSpec((tile, dim), lambda j: (j, 0)),
            line,
        ],
        out_specs=[line, line, line, line],
        out_shape=[jax.ShapeDtypeStruct((1, count), jnp.float32)] * 4,
        cost_estimate=pl.CostEstimate(
            flops=2 * count * width * dim,
            transcendentals=count * width,
            bytes_accessed=2 * (count + width) * dim,
        ),
    )(rows, vocab, spot.reshape(1, count))
    return tuple(o.reshape(count) for o in outs)


def on_device(hidden, norm_gain, unembed, targets, live):
    ny = lax.axis_size("y")
    nc = lax.axis_size("c")
    y = lax.axis_index("y")
    c = lax.axis_index("c")
    mine = hidden.shape[0]
    dim = hidden.shape[1]
    width = unembed.shape[0]

    wide = hidden.astype(jnp.float32)
    normed = (
        wide * lax.rsqrt(jnp.mean(wide * wide, axis=1, keepdims=True) + 1e-06) * norm_gain
    ).astype(jnp.bfloat16)

    code = jnp.zeros((mine, 16), jnp.bfloat16)
    code = code.at[:, 0].set((targets // 128).astype(jnp.bfloat16))
    code = code.at[:, 1].set((targets % 128).astype(jnp.bfloat16))
    block = jnp.concatenate([normed, code], axis=1)

    nx = lax.axis_size("x")
    x = lax.axis_index("x")
    near = [unembed] + [shift(unembed, "x", nx, -d) for d in range(1, nx)]
    block, *rest = lax.optimization_barrier((block, *near[1:]))
    near[1:] = rest

    blocks = [None] * ny
    blocks[0] = block
    half = ny // 2
    fronts = {}
    for sign in (1, -1):
        cur = block
        for step in range(1, half):
            cur = shift(cur, "y", ny, sign)
            blocks[(-sign * step) % ny] = cur
        fronts[sign] = cur
    if ny % 2 == 0:
        cut = mine // 2
        first = shift(fronts[1][:cut], "y", ny, 1)
        second = shift(fronts[-1][cut:], "y", ny, -1)
        blocks[half] = jnp.concatenate([first, second], axis=0)
    rows = jnp.concatenate([b[:, :dim] for b in blocks], axis=0)
    wanted = jnp.concatenate(
        [b[:, dim].astype(jnp.int32) * 128 + b[:, dim + 1].astype(jnp.int32) for b in blocks], axis=0
    )

    whole = lax.all_gather(jnp.concatenate(near, axis=0), ("z", "c"), axis=0, tiled=True)
    owner, entry = wanted // width, wanted % width
    req, shard = owner // ny, owner % ny
    far_c, far_x, far_z = req % nc, (req // nc) % nx, req // (nc * nx)
    spot = ((far_z * nc + far_c) * nx + (far_x - x) % nx) * width + entry
    spot = jnp.where(shard == y, spot, -1)

    stats = row_stats(rows, whole, spot)

    packed = jnp.roll(jnp.stack(stats).reshape(4, ny, mine), y, axis=1).reshape(4, ny * mine)
    got = lax.all_to_all(packed, "y", 1, 1, tiled=True).reshape(4, ny, mine)
    tops, totals, spreads, chosen = got[0], got[1], got[2], got[3]
    top = jnp.max(tops, axis=0)
    scale = jnp.exp(tops - top[None])
    total = jnp.sum(totals * scale, axis=0)
    spread = jnp.sum(scale * (spreads + (tops - top[None]) * totals), axis=0)
    picked = jnp.sum(chosen, axis=0)
    mask = live.astype(jnp.float32)
    logprob = (picked - top - jnp.log(total)) * mask
    entropy = (jnp.log(total) - spread / total) * mask
    return (logprob, entropy)


def solution(mesh):
    nz, nx, nc = 8, 4, 2
    ny = mesh.devices.shape[1]
    req = mesh.devices.shape[0]
    nz = req // (nx * nc)
    flat = Mesh(mesh.devices.reshape(nz, nx, nc, ny), FLAT)
    return jax.shard_map(
        on_device,
        mesh=flat,
        in_specs=(P(FLAT, None), P(), P(FLAT, None), P(FLAT), P(FLAT)),
        out_specs=(P(FLAT), P(FLAT)),
        check_vma=False,
    )
```

```python
import functools

import jax
import jax.numpy as jnp
from jax import lax
from jax.experimental import pallas as pl
from jax.experimental.pallas import tpu as pltpu
from jax.sharding import Mesh, PartitionSpec as P

FLAT = ("z", "x", "c", "y")


def combine_stats(first, second):
    top = jnp.maximum(first[0], second[0])
    scale_one = jnp.exp(first[0] - top)
    scale_two = jnp.exp(second[0] - top)
    total = first[1] * scale_one + second[1] * scale_two
    spread = scale_one * (first[2] + (first[0] - top) * first[1]) + scale_two * (
        second[2] + (second[0] - top) * second[1]
    )
    return (top, total, spread, first[3] + second[3])


def shift(value, axis, size, step):
    return lax.ppermute(value, axis, [(i, (i + step) % size) for i in range(size)])


def chunk_stats(normed, piece, ids, wanted):
    logits = lax.dot_general(
        normed, piece, (((1,), (1,)), ((), ())), preferred_element_type=jnp.float32
    )
    chosen = jnp.sum(jnp.where(ids[None, :] == wanted[:, None], logits, 0.0), axis=1)
    fold_top = jnp.max(logits, axis=1)
    shifted = logits - fold_top[:, None]
    weights = jnp.exp(shifted)
    return (fold_top, jnp.sum(weights, axis=1), jnp.sum(weights * shifted, axis=1), chosen)


def stats_kernel(parts, dim, *refs):
    block_refs = refs[:parts]
    vocab_ref, spot_ref, top_ref, total_ref, spread_ref, chosen_ref, rows_ref = refs[parts:]
    j = pl.program_id(0)
    tile = vocab_ref.shape[0]
    position = j * tile + lax.broadcasted_iota(jnp.int32, (tile, 1), 0)

    @pl.when(j == 0)
    def _():
        size = block_refs[0].shape[0]
        for b, block_ref in enumerate(block_refs):
            rows_ref[b * size : (b + 1) * size, :] = block_ref[:, :dim]
        top_ref[...] = jnp.full(top_ref.shape, -1e30, jnp.float32)
        total_ref[...] = jnp.zeros(total_ref.shape, jnp.float32)
        spread_ref[...] = jnp.zeros(spread_ref.shape, jnp.float32)
        chosen_ref[...] = jnp.zeros(chosen_ref.shape, jnp.float32)

    logits = lax.dot_general(
        vocab_ref[...], rows_ref[...], (((1,), (1,)), ((), ())), preferred_element_type=jnp.float32
    )
    hit = position == spot_ref[...]
    chosen_ref[...] += jnp.sum(jnp.where(hit, logits, 0.0), axis=0, keepdims=True)
    fold = jnp.max(logits, axis=0, keepdims=True)
    shifted = logits - fold
    weights = jnp.exp(shifted)
    new_total = jnp.sum(weights, axis=0, keepdims=True)
    new_spread = jnp.sum(weights * shifted, axis=0, keepdims=True)
    old_top = top_ref[...]
    top = jnp.maximum(old_top, fold)
    scale_one = jnp.exp(old_top - top)
    scale_two = jnp.exp(fold - top)
    old_total = total_ref[...]
    total_ref[...] = old_total * scale_one + new_total * scale_two
    spread_ref[...] = scale_one * (spread_ref[...] + (old_top - top) * old_total) + scale_two * (
        new_spread + (fold - top) * new_total
    )
    top_ref[...] = top


def row_stats(blocks, dim, vocab, spot, tile=512):
    size = blocks[0].shape[0]
    count = size * len(blocks)
    width = vocab.shape[0]
    line = pl.BlockSpec((1, count), lambda j: (0, 0))
    whole_block = pl.BlockSpec(blocks[0].shape, lambda j: (0, 0))
    outs = pl.pallas_call(
        functools.partial(stats_kernel, len(blocks), dim),
        grid=(width // tile,),
        in_specs=[whole_block] * len(blocks) + [pl.BlockSpec((tile, dim), lambda j: (j, 0)), line],
        out_specs=[line, line, line, line],
        out_shape=[jax.ShapeDtypeStruct((1, count), jnp.float32)] * 4,
        scratch_shapes=[pltpu.VMEM((count, dim), blocks[0].dtype)],
        cost_estimate=pl.CostEstimate(
            flops=2 * count * width * dim,
            transcendentals=count * width,
            bytes_accessed=2 * (count + width) * dim,
        ),
    )(*blocks, vocab, spot.reshape(1, count))
    return tuple(o.reshape(count) for o in outs)


def on_device(hidden, norm_gain, unembed, targets, live):
    ny = lax.axis_size("y")
    nc = lax.axis_size("c")
    y = lax.axis_index("y")
    c = lax.axis_index("c")
    mine = hidden.shape[0]
    dim = hidden.shape[1]
    width = unembed.shape[0]

    wide = hidden.astype(jnp.float32)
    normed = (
        wide * lax.rsqrt(jnp.mean(wide * wide, axis=1, keepdims=True) + 1e-06) * norm_gain
    ).astype(jnp.bfloat16)

    code = jnp.zeros((mine, 16), jnp.bfloat16)
    code = code.at[:, 0].set((targets // 128).astype(jnp.bfloat16))
    code = code.at[:, 1].set((targets % 128).astype(jnp.bfloat16))
    block = jnp.concatenate([normed, code], axis=1)

    nx = lax.axis_size("x")
    x = lax.axis_index("x")
    near = [unembed] + [shift(unembed, "x", nx, -d) for d in range(1, nx)]
    block, *rest = lax.optimization_barrier((block, *near[1:]))
    near[1:] = rest

    blocks = [None] * ny
    blocks[0] = block
    for sign in (1, -1):
        cur = block
        reach = ny // 2 if sign == 1 else ny - 1 - ny // 2
        for step in range(1, reach + 1):
            cur = shift(cur, "y", ny, sign)
            blocks[(-sign * step) % ny] = cur
    wanted = jnp.concatenate(
        [b[:, dim].astype(jnp.int32) * 128 + b[:, dim + 1].astype(jnp.int32) for b in blocks], axis=0
    )

    whole = lax.all_gather(jnp.concatenate(near, axis=0), ("z", "c"), axis=0, tiled=True)
    owner, entry = wanted // width, wanted % width
    req, shard = owner // ny, owner % ny
    far_c, far_x, far_z = req % nc, (req // nc) % nx, req // (nc * nx)
    spot = ((far_z * nc + far_c) * nx + (far_x - x) % nx) * width + entry
    spot = jnp.where(shard == y, spot, -1)

    stats = row_stats(blocks, dim, whole, spot)

    packed = jnp.roll(jnp.stack(stats).reshape(4, ny, mine), y, axis=1).reshape(4, ny * mine)
    got = lax.all_to_all(packed, "y", 1, 1, tiled=True).reshape(4, ny, mine)
    tops, totals, spreads, chosen = got[0], got[1], got[2], got[3]
    top = jnp.max(tops, axis=0)
    scale = jnp.exp(tops - top[None])
    total = jnp.sum(totals * scale, axis=0)
    spread = jnp.sum(scale * (spreads + (tops - top[None]) * totals), axis=0)
    picked = jnp.sum(chosen, axis=0)
    mask = live.astype(jnp.float32)
    logprob = (picked - top - jnp.log(total)) * mask
    entropy = (jnp.log(total) - spread / total) * mask
    return (logprob, entropy)


def solution(mesh):
    nz, nx, nc = 8, 4, 2
    ny = mesh.devices.shape[1]
    req = mesh.devices.shape[0]
    nz = req // (nx * nc)
    flat = Mesh(mesh.devices.reshape(nz, nx, nc, ny), FLAT)
    return jax.shard_map(
        on_device,
        mesh=flat,
        in_specs=(P(FLAT, None), P(), P(FLAT, None), P(FLAT), P(FLAT)),
        out_specs=(P(FLAT), P(FLAT)),
        check_vma=False,
    )
```

```python
import functools

import jax
import jax.numpy as jnp
from jax import lax
from jax.experimental import pallas as pl
from jax.experimental.pallas import tpu as pltpu
from jax.sharding import Mesh, PartitionSpec as P

FLAT = ("z", "x", "c", "y")


def combine_stats(first, second):
    top = jnp.maximum(first[0], second[0])
    scale_one = jnp.exp(first[0] - top)
    scale_two = jnp.exp(second[0] - top)
    total = first[1] * scale_one + second[1] * scale_two
    spread = scale_one * (first[2] + (first[0] - top) * first[1]) + scale_two * (
        second[2] + (second[0] - top) * second[1]
    )
    return (top, total, spread, first[3] + second[3])


def shift(value, axis, size, step):
    return lax.ppermute(value, axis, [(i, (i + step) % size) for i in range(size)])


def chunk_stats(normed, piece, ids, wanted):
    logits = lax.dot_general(
        normed, piece, (((1,), (1,)), ((), ())), preferred_element_type=jnp.float32
    )
    chosen = jnp.sum(jnp.where(ids[None, :] == wanted[:, None], logits, 0.0), axis=1)
    fold_top = jnp.max(logits, axis=1)
    shifted = logits - fold_top[:, None]
    weights = jnp.exp(shifted)
    return (fold_top, jnp.sum(weights, axis=1), jnp.sum(weights * shifted, axis=1), chosen)


def stats_kernel(parts, dim, *refs):
    block_refs = refs[:parts]
    vocab_ref, spot_ref, top_ref, total_ref, spread_ref, chosen_ref, rows_ref = refs[parts:]
    j = pl.program_id(0)
    tile = vocab_ref.shape[0]
    position = j * tile + lax.broadcasted_iota(jnp.int32, (tile, 1), 0)

    @pl.when(j == 0)
    def _():
        size = block_refs[0].shape[0]
        for b, block_ref in enumerate(block_refs):
            rows_ref[b * size : (b + 1) * size, :] = block_ref[:, :dim]
        top_ref[...] = jnp.full(top_ref.shape, -1e30, jnp.float32)
        total_ref[...] = jnp.zeros(total_ref.shape, jnp.float32)
        spread_ref[...] = jnp.zeros(spread_ref.shape, jnp.float32)
        chosen_ref[...] = jnp.zeros(chosen_ref.shape, jnp.float32)

    logits = lax.dot_general(
        vocab_ref[...], rows_ref[...], (((1,), (1,)), ((), ())), preferred_element_type=jnp.float32
    )
    hit = position == spot_ref[...]
    chosen_ref[...] += jnp.sum(jnp.where(hit, logits, 0.0), axis=0, keepdims=True)
    fold = jnp.max(logits, axis=0, keepdims=True)
    shifted = logits - fold
    weights = jnp.exp(shifted)
    new_total = jnp.sum(weights, axis=0, keepdims=True)
    new_spread = jnp.sum(weights * shifted, axis=0, keepdims=True)
    old_top = top_ref[...]
    top = jnp.maximum(old_top, fold)
    scale_one = jnp.exp(old_top - top)
    scale_two = jnp.exp(fold - top)
    old_total = total_ref[...]
    total_ref[...] = old_total * scale_one + new_total * scale_two
    spread_ref[...] = scale_one * (spread_ref[...] + (old_top - top) * old_total) + scale_two * (
        new_spread + (fold - top) * new_total
    )
    top_ref[...] = top


def row_stats(blocks, dim, vocab, spot, tile=512):
    size = blocks[0].shape[0]
    count = size * len(blocks)
    width = vocab.shape[0]
    line = pl.BlockSpec((1, count), lambda j: (0, 0))
    whole_block = pl.BlockSpec(blocks[0].shape, lambda j: (0, 0))
    outs = pl.pallas_call(
        functools.partial(stats_kernel, len(blocks), dim),
        grid=(width // tile,),
        in_specs=[whole_block] * len(blocks) + [pl.BlockSpec((tile, dim), lambda j: (j, 0)), line],
        out_specs=[line, line, line, line],
        out_shape=[jax.ShapeDtypeStruct((1, count), jnp.float32)] * 4,
        scratch_shapes=[pltpu.VMEM((count, dim), blocks[0].dtype)],
        cost_estimate=pl.CostEstimate(
            flops=2 * count * width * dim,
            transcendentals=count * width,
            bytes_accessed=2 * (count + width) * dim,
        ),
    )(*blocks, vocab, spot.reshape(1, count))
    return tuple(o.reshape(count) for o in outs)


def on_device(hidden, norm_gain, unembed, targets, live):
    ny = lax.axis_size("y")
    nc = lax.axis_size("c")
    y = lax.axis_index("y")
    c = lax.axis_index("c")
    mine = hidden.shape[0]
    dim = hidden.shape[1]
    width = unembed.shape[0]

    wide = hidden.astype(jnp.float32)
    normed = (
        wide * lax.rsqrt(jnp.mean(wide * wide, axis=1, keepdims=True) + 1e-06) * norm_gain
    ).astype(jnp.bfloat16)

    code = jnp.zeros((mine, 16), jnp.bfloat16)
    code = code.at[:, 0].set((targets // 128).astype(jnp.bfloat16))
    code = code.at[:, 1].set((targets % 128).astype(jnp.bfloat16))
    block = jnp.concatenate([normed, code], axis=1)

    nx = lax.axis_size("x")
    x = lax.axis_index("x")
    near = [unembed] + [shift(unembed, "x", nx, -d) for d in range(1, nx)]
    table = jnp.concatenate(near, axis=0)
    block, _ = lax.optimization_barrier((block, table))

    blocks = [None] * ny
    blocks[0] = block
    for sign in (1, -1):
        cur = block
        reach = ny // 2 if sign == 1 else ny - 1 - ny // 2
        for step in range(1, reach + 1):
            cur = shift(cur, "y", ny, sign)
            blocks[(-sign * step) % ny] = cur
    wanted = jnp.concatenate(
        [b[:, dim].astype(jnp.int32) * 128 + b[:, dim + 1].astype(jnp.int32) for b in blocks], axis=0
    )

    whole = lax.all_gather(table, ("z", "c"), axis=0, tiled=True)
    owner, entry = wanted // width, wanted % width
    req, shard = owner // ny, owner % ny
    far_c, far_x, far_z = req % nc, (req // nc) % nx, req // (nc * nx)
    spot = ((far_z * nc + far_c) * nx + (far_x - x) % nx) * width + entry
    spot = jnp.where(shard == y, spot, -1)

    stats = row_stats(blocks, dim, whole, spot)

    packed = jnp.roll(jnp.stack(stats).reshape(4, ny, mine), y, axis=1).reshape(4, ny * mine)
    got = lax.all_to_all(packed, "y", 1, 1, tiled=True).reshape(4, ny, mine)
    tops, totals, spreads, chosen = got[0], got[1], got[2], got[3]
    top = jnp.max(tops, axis=0)
    scale = jnp.exp(tops - top[None])
    total = jnp.sum(totals * scale, axis=0)
    spread = jnp.sum(scale * (spreads + (tops - top[None]) * totals), axis=0)
    picked = jnp.sum(chosen, axis=0)
    mask = live.astype(jnp.float32)
    logprob = (picked - top - jnp.log(total)) * mask
    entropy = (jnp.log(total) - spread / total) * mask
    return (logprob, entropy)


def solution(mesh):
    nz, nx, nc = 8, 4, 2
    ny = mesh.devices.shape[1]
    req = mesh.devices.shape[0]
    nz = req // (nx * nc)
    flat = Mesh(mesh.devices.reshape(nz, nx, nc, ny), FLAT)
    return jax.shard_map(
        on_device,
        mesh=flat,
        in_specs=(P(FLAT, None), P(), P(FLAT, None), P(FLAT), P(FLAT)),
        out_specs=(P(FLAT), P(FLAT)),
        check_vma=False,
    )
```

```python
import functools

import jax
import jax.numpy as jnp
from jax import lax
from jax.experimental import pallas as pl
from jax.experimental.pallas import tpu as pltpu
from jax.sharding import Mesh, PartitionSpec as P

FLAT = ("z", "x", "c", "y")


def combine_stats(first, second):
    top = jnp.maximum(first[0], second[0])
    scale_one = jnp.exp(first[0] - top)
    scale_two = jnp.exp(second[0] - top)
    total = first[1] * scale_one + second[1] * scale_two
    spread = scale_one * (first[2] + (first[0] - top) * first[1]) + scale_two * (
        second[2] + (second[0] - top) * second[1]
    )
    return (top, total, spread, first[3] + second[3])


def shift(value, axis, size, step):
    return lax.ppermute(value, axis, [(i, (i + step) % size) for i in range(size)])


def chunk_stats(normed, piece, ids, wanted):
    logits = lax.dot_general(
        normed, piece, (((1,), (1,)), ((), ())), preferred_element_type=jnp.float32
    )
    chosen = jnp.sum(jnp.where(ids[None, :] == wanted[:, None], logits, 0.0), axis=1)
    fold_top = jnp.max(logits, axis=1)
    shifted = logits - fold_top[:, None]
    weights = jnp.exp(shifted)
    return (fold_top, jnp.sum(weights, axis=1), jnp.sum(weights * shifted, axis=1), chosen)


def stats_kernel(parts, dim, *refs):
    block_refs = refs[:parts]
    vocab_ref, spot_ref, top_ref, total_ref, spread_ref, chosen_ref, rows_ref = refs[parts:]
    j = pl.program_id(0)
    tile = vocab_ref.shape[0]
    position = j * tile + lax.broadcasted_iota(jnp.int32, (tile, 1), 0)

    @pl.when(j == 0)
    def _():
        size = block_refs[0].shape[0]
        for b, block_ref in enumerate(block_refs):
            rows_ref[b * size : (b + 1) * size, :] = block_ref[:, :dim]
        top_ref[...] = jnp.full(top_ref.shape, -1e30, jnp.float32)
        total_ref[...] = jnp.zeros(total_ref.shape, jnp.float32)
        spread_ref[...] = jnp.zeros(spread_ref.shape, jnp.float32)
        chosen_ref[...] = jnp.zeros(chosen_ref.shape, jnp.float32)

    logits = lax.dot_general(
        vocab_ref[...], rows_ref[...], (((1,), (1,)), ((), ())), preferred_element_type=jnp.float32
    )
    hit = position == spot_ref[...]
    chosen_ref[...] += jnp.sum(jnp.where(hit, logits, 0.0), axis=0, keepdims=True)
    fold = jnp.max(logits, axis=0, keepdims=True)
    shifted = logits - fold
    weights = jnp.exp(shifted)
    new_total = jnp.sum(weights, axis=0, keepdims=True)
    new_spread = jnp.sum(weights * shifted, axis=0, keepdims=True)
    old_top = top_ref[...]
    top = jnp.maximum(old_top, fold)
    scale_one = jnp.exp(old_top - top)
    scale_two = jnp.exp(fold - top)
    old_total = total_ref[...]
    total_ref[...] = old_total * scale_one + new_total * scale_two
    spread_ref[...] = scale_one * (spread_ref[...] + (old_top - top) * old_total) + scale_two * (
        new_spread + (fold - top) * new_total
    )
    top_ref[...] = top


def row_stats(blocks, dim, vocab, spot, tile=1024):
    size = blocks[0].shape[0]
    count = size * len(blocks)
    width = vocab.shape[0]
    line = pl.BlockSpec((1, count), lambda j: (0, 0))
    whole_block = pl.BlockSpec(blocks[0].shape, lambda j: (0, 0))
    outs = pl.pallas_call(
        functools.partial(stats_kernel, len(blocks), dim),
        grid=(width // tile,),
        in_specs=[whole_block] * len(blocks) + [pl.BlockSpec((tile, dim), lambda j: (j, 0)), line],
        out_specs=[line, line, line, line],
        out_shape=[jax.ShapeDtypeStruct((1, count), jnp.float32)] * 4,
        scratch_shapes=[pltpu.VMEM((count, dim), blocks[0].dtype)],
        cost_estimate=pl.CostEstimate(
            flops=2 * count * width * dim,
            transcendentals=count * width,
            bytes_accessed=2 * (count + width) * dim,
        ),
    )(*blocks, vocab, spot.reshape(1, count))
    return tuple(o.reshape(count) for o in outs)


def on_device(hidden, norm_gain, unembed, targets, live):
    ny = lax.axis_size("y")
    nc = lax.axis_size("c")
    y = lax.axis_index("y")
    c = lax.axis_index("c")
    mine = hidden.shape[0]
    dim = hidden.shape[1]
    width = unembed.shape[0]

    wide = hidden.astype(jnp.float32)
    normed = (
        wide * lax.rsqrt(jnp.mean(wide * wide, axis=1, keepdims=True) + 1e-06) * norm_gain
    ).astype(jnp.bfloat16)

    code = jnp.zeros((mine, 16), jnp.bfloat16)
    code = code.at[:, 0].set((targets // 128).astype(jnp.bfloat16))
    code = code.at[:, 1].set((targets % 128).astype(jnp.bfloat16))
    block = jnp.concatenate([normed, code], axis=1)

    nx = lax.axis_size("x")
    x = lax.axis_index("x")
    near = [unembed] + [shift(unembed, "x", nx, -d) for d in range(1, nx)]
    table = jnp.concatenate(near, axis=0)
    block, _ = lax.optimization_barrier((block, table))

    blocks = [None] * ny
    blocks[0] = block
    for sign in (1, -1):
        cur = block
        reach = ny // 2 if sign == 1 else ny - 1 - ny // 2
        for step in range(1, reach + 1):
            cur = shift(cur, "y", ny, sign)
            blocks[(-sign * step) % ny] = cur
    wanted = jnp.concatenate(
        [b[:, dim].astype(jnp.int32) * 128 + b[:, dim + 1].astype(jnp.int32) for b in blocks], axis=0
    )

    whole = lax.all_gather(table, ("z", "c"), axis=0, tiled=True)
    owner, entry = wanted // width, wanted % width
    req, shard = owner // ny, owner % ny
    far_c, far_x, far_z = req % nc, (req // nc) % nx, req // (nc * nx)
    spot = ((far_z * nc + far_c) * nx + (far_x - x) % nx) * width + entry
    spot = jnp.where(shard == y, spot, -1)

    stats = row_stats(blocks, dim, whole, spot)

    packed = jnp.roll(jnp.stack(stats).reshape(4, ny, mine), y, axis=1).reshape(4, ny * mine)
    got = lax.all_to_all(packed, "y", 1, 1, tiled=True).reshape(4, ny, mine)
    tops, totals, spreads, chosen = got[0], got[1], got[2], got[3]
    top = jnp.max(tops, axis=0)
    scale = jnp.exp(tops - top[None])
    total = jnp.sum(totals * scale, axis=0)
    spread = jnp.sum(scale * (spreads + (tops - top[None]) * totals), axis=0)
    picked = jnp.sum(chosen, axis=0)
    mask = live.astype(jnp.float32)
    logprob = (picked - top - jnp.log(total)) * mask
    entropy = (jnp.log(total) - spread / total) * mask
    return (logprob, entropy)


def solution(mesh):
    nz, nx, nc = 8, 4, 2
    ny = mesh.devices.shape[1]
    req = mesh.devices.shape[0]
    nz = req // (nx * nc)
    flat = Mesh(mesh.devices.reshape(nz, nx, nc, ny), FLAT)
    return jax.shard_map(
        on_device,
        mesh=flat,
        in_specs=(P(FLAT, None), P(), P(FLAT, None), P(FLAT), P(FLAT)),
        out_specs=(P(FLAT), P(FLAT)),
        check_vma=False,
    )
```

```python
import functools

import jax
import jax.numpy as jnp
from jax import lax
from jax.experimental import pallas as pl
from jax.experimental.pallas import tpu as pltpu
from jax.sharding import Mesh, PartitionSpec as P

FLAT = ("z", "x", "c", "y")


def combine_stats(first, second):
    top = jnp.maximum(first[0], second[0])
    scale_one = jnp.exp(first[0] - top)
    scale_two = jnp.exp(second[0] - top)
    total = first[1] * scale_one + second[1] * scale_two
    spread = scale_one * (first[2] + (first[0] - top) * first[1]) + scale_two * (
        second[2] + (second[0] - top) * second[1]
    )
    return (top, total, spread, first[3] + second[3])


def shift(value, axis, size, step):
    return lax.ppermute(value, axis, [(i, (i + step) % size) for i in range(size)])


def chunk_stats(normed, piece, ids, wanted):
    logits = lax.dot_general(
        normed, piece, (((1,), (1,)), ((), ())), preferred_element_type=jnp.float32
    )
    chosen = jnp.sum(jnp.where(ids[None, :] == wanted[:, None], logits, 0.0), axis=1)
    fold_top = jnp.max(logits, axis=1)
    shifted = logits - fold_top[:, None]
    weights = jnp.exp(shifted)
    return (fold_top, jnp.sum(weights, axis=1), jnp.sum(weights * shifted, axis=1), chosen)


def stats_kernel(parts, dim, *refs):
    block_refs = refs[:parts]
    where_ref, vocab_ref, spot_ref, top_ref, total_ref, spread_ref, chosen_ref, rows_ref = refs[parts:]
    j = pl.program_id(0)
    tile = vocab_ref.shape[0]
    position = j * tile + lax.broadcasted_iota(jnp.int32, (tile, 1), 0)

    @pl.when(j == 0)
    def _():
        size = block_refs[0].shape[0]
        for b, block_ref in enumerate(block_refs):
            place = pl.multiple_of(((where_ref[0] + b) % parts) * size, size)
            rows_ref[pl.ds(place, size), :] = block_ref[:, :dim]
        top_ref[...] = jnp.full(top_ref.shape, -1e30, jnp.float32)
        total_ref[...] = jnp.zeros(total_ref.shape, jnp.float32)
        spread_ref[...] = jnp.zeros(spread_ref.shape, jnp.float32)
        chosen_ref[...] = jnp.zeros(chosen_ref.shape, jnp.float32)

    logits = lax.dot_general(
        vocab_ref[...], rows_ref[...], (((1,), (1,)), ((), ())), preferred_element_type=jnp.float32
    )
    hit = position == spot_ref[...]
    chosen_ref[...] += jnp.sum(jnp.where(hit, logits, 0.0), axis=0, keepdims=True)
    fold = jnp.max(logits, axis=0, keepdims=True)
    shifted = logits - fold
    weights = jnp.exp(shifted)
    new_total = jnp.sum(weights, axis=0, keepdims=True)
    new_spread = jnp.sum(weights * shifted, axis=0, keepdims=True)
    old_top = top_ref[...]
    top = jnp.maximum(old_top, fold)
    scale_one = jnp.exp(old_top - top)
    scale_two = jnp.exp(fold - top)
    old_total = total_ref[...]
    total_ref[...] = old_total * scale_one + new_total * scale_two
    spread_ref[...] = scale_one * (spread_ref[...] + (old_top - top) * old_total) + scale_two * (
        new_spread + (fold - top) * new_total
    )
    top_ref[...] = top


def row_stats(blocks, dim, where, vocab, spot, tile=512):
    size = blocks[0].shape[0]
    count = size * len(blocks)
    width = vocab.shape[0]
    line = pl.BlockSpec((1, count), lambda j: (0, 0))
    whole_block = pl.BlockSpec(blocks[0].shape, lambda j: (0, 0))
    outs = pl.pallas_call(
        functools.partial(stats_kernel, len(blocks), dim),
        grid=(width // tile,),
        in_specs=[whole_block] * len(blocks)
        + [pl.BlockSpec(memory_space=pltpu.SMEM), pl.BlockSpec((tile, dim), lambda j: (j, 0)), line],
        out_specs=[line, line, line, line],
        out_shape=[jax.ShapeDtypeStruct((1, count), jnp.float32)] * 4,
        scratch_shapes=[pltpu.VMEM((count, dim), blocks[0].dtype)],
        cost_estimate=pl.CostEstimate(
            flops=2 * count * width * dim,
            transcendentals=count * width,
            bytes_accessed=2 * (count + width) * dim,
        ),
    )(*blocks, where, vocab, spot.reshape(1, count))
    return tuple(o.reshape(count) for o in outs)


def on_device(hidden, norm_gain, unembed, targets, live):
    ny = lax.axis_size("y")
    nc = lax.axis_size("c")
    y = lax.axis_index("y")
    c = lax.axis_index("c")
    mine = hidden.shape[0]
    dim = hidden.shape[1]
    width = unembed.shape[0]

    wide = hidden.astype(jnp.float32)
    normed = (
        wide * lax.rsqrt(jnp.mean(wide * wide, axis=1, keepdims=True) + 1e-06) * norm_gain
    ).astype(jnp.bfloat16)

    code = jnp.zeros((mine, 16), jnp.bfloat16)
    code = code.at[:, 0].set((targets // 128).astype(jnp.bfloat16))
    code = code.at[:, 1].set((targets % 128).astype(jnp.bfloat16))
    block = jnp.concatenate([normed, code], axis=1)

    nx = lax.axis_size("x")
    x = lax.axis_index("x")
    near = [unembed] + [shift(unembed, "x", nx, -d) for d in range(1, nx)]
    table = jnp.concatenate(near, axis=0)
    block, _ = lax.optimization_barrier((block, table))

    blocks = [None] * ny
    blocks[0] = block
    for sign in (1, -1):
        cur = block
        reach = ny // 2 if sign == 1 else ny - 1 - ny // 2
        for step in range(1, reach + 1):
            cur = shift(cur, "y", ny, sign)
            blocks[(-sign * step) % ny] = cur
    wanted = jnp.concatenate(
        [b[:, dim].astype(jnp.int32) * 128 + b[:, dim + 1].astype(jnp.int32) for b in blocks], axis=0
    )

    whole = lax.all_gather(table, ("z", "c"), axis=0, tiled=True)
    owner, entry = wanted // width, wanted % width
    req, shard = owner // ny, owner % ny
    far_c, far_x, far_z = req % nc, (req // nc) % nx, req // (nc * nx)
    spot = ((far_z * nc + far_c) * nx + (far_x - x) % nx) * width + entry
    spot = jnp.where(shard == y, spot, -1)

    spot = jnp.roll(spot, y * mine)
    stats = row_stats(blocks, dim, y.astype(jnp.int32).reshape(1), whole, spot)

    packed = jnp.stack(stats)
    got = lax.all_to_all(packed, "y", 1, 1, tiled=True).reshape(4, ny, mine)
    tops, totals, spreads, chosen = got[0], got[1], got[2], got[3]
    top = jnp.max(tops, axis=0)
    scale = jnp.exp(tops - top[None])
    total = jnp.sum(totals * scale, axis=0)
    spread = jnp.sum(scale * (spreads + (tops - top[None]) * totals), axis=0)
    picked = jnp.sum(chosen, axis=0)
    mask = live.astype(jnp.float32)
    logprob = (picked - top - jnp.log(total)) * mask
    entropy = (jnp.log(total) - spread / total) * mask
    return (logprob, entropy)


def solution(mesh):
    nz, nx, nc = 8, 4, 2
    ny = mesh.devices.shape[1]
    req = mesh.devices.shape[0]
    nz = req // (nx * nc)
    flat = Mesh(mesh.devices.reshape(nz, nx, nc, ny), FLAT)
    return jax.shard_map(
        on_device,
        mesh=flat,
        in_specs=(P(FLAT, None), P(), P(FLAT, None), P(FLAT), P(FLAT)),
        out_specs=(P(FLAT), P(FLAT)),
        check_vma=False,
    )
```
